32 devices in a mesh: rep: 4 (over x, core), frame: 4 (over z), row: 2 (over y).
Axes of the slice: x: 2, y: 2, z: 4, core: 2. Of those that a mesh axis runs over, the one named last changes fastest.
Arguments:
- activations: bfloat16 [4, 4, 16, 32, 1280], P('rep', 'frame', 'row'), may hold values from -70 to 70, as said below
- spatial_weight: bfloat16 [9, 1280, 1280], P(None, None, ('rep', 'frame')), may hold values from -0.0546875 to 0.0546875
- temporal_weight: bfloat16 [3, 1280, 1280], P(None, None, ('rep', 'frame')), may hold values from -0.09375 to 0.09375
- first_gain: float32 [1280], replicated, may hold values from 0.25 to 1.75
- first_shift: float32 [1280], replicated, may hold values from -1.5 to 1.5
- spatial_bias: float32 [1280], replicated, may hold values from -2.5 to 2.5
- second_gain: float32 [1280], replicated, may hold values from 0.25 to 1.75
- second_shift: float32 [1280], replicated, may hold values from -1.5 to 1.5
- temporal_bias: float32 [1280], replicated, may hold values from -1.5 to 1.5
Outputs:
- block_out: float32 [4, 4, 16, 32, 1280], P('rep', 'frame', 'row')
The draws below stay inside these ranges and needn't reach their ends.
Inputs may be any that keep to these rules, and one draw needn't show every extreme that they name: `activations`: finite values.
All inputs are finite; a program needn't handle non-finite values.
Results may differ from the reference program's by a relative error of at most 0.0009.
Values may be sent and summed in bfloat16 or wider, within the bound.
No kernel may reach another device: no remote copies, remote signals or barrier semaphores. Data moves between devices by JAX's collectives and lax.ppermute only.
A program may use at most 128 MiB of HBM per device.

```python
import math
import jax
import jax.numpy as jnp
from jax import lax

CHANNELS = 1280
GROUPS = 32
COLS = 32
BATCH = 4
FRAMES = 4
ROWS = 16


def draw_activations(key, part):
    first_key, second_key = jax.random.split(jax.random.fold_in(key, 17), 2)
    shape = (BATCH, FRAMES, ROWS, COLS, CHANNELS)
    position = jnp.arange(FRAMES, dtype=jnp.float32) / max(FRAMES - 1, 1)
    frame_scale = jnp.sqrt(1.0 + 2.0 * position)[None, :, None, None, None]
    channel_scale = jnp.exp(jax.random.uniform(second_key, (CHANNELS,), jnp.float32, 0.0, math.log(10.0)))
    base = jnp.clip(jax.random.normal(first_key, shape, jnp.float32), -4.0, 4.0)
    return (base * frame_scale * channel_scale).astype(jnp.bfloat16)


def shard_levels(own_key, extent, pieces, least, high):
    loudness, own = 1.0, jax.random.fold_in(own_key, 6)
    for axis_at, blocks in pieces:
        heights = jnp.exp(jax.random.uniform(jax.random.fold_in(own, axis_at), (blocks,), jnp.float32, least / len(pieces), high / len(pieces)))
        loudness = loudness * jnp.repeat(heights, extent[axis_at] // blocks).reshape([-1 if axis == axis_at else 1 for axis in range(len(extent))])
    return loudness


def normal_values(stream_key, extent, scale, bound, cuts=(), kind=jnp.bfloat16):
    array = jax.random.normal(stream_key, extent, jnp.float32) * scale
    if len(cuts) > 0:
        array = shard_levels(stream_key, extent, cuts, -0.22, 0.18) * array
    return jnp.clip(array, min=-bound, max=bound).astype(kind)


def setup_inputs(seed: int = 0) -> dict:
    splits = jax.random.split(jax.random.key(seed), 10)
    activations = draw_activations(jax.random.fold_in(splits[9], 71), 0)
    spatial_weight = normal_values(splits[1], (9, CHANNELS, CHANNELS), (9 * CHANNELS) ** -0.5, 0.0546875, ((2, 16),))
    temporal_weight = normal_values(splits[2], (3, CHANNELS, CHANNELS), (3 * CHANNELS) ** -0.5, 0.09375, ((2, 16),))
    first_gain = jnp.clip(1.0 + 0.15 * jax.random.normal(splits[3], (CHANNELS,), jnp.float32), 0.25, 1.75)
    first_shift = normal_values(splits[4], (CHANNELS,), 0.3, 1.5, (), jnp.float32)
    spatial_bias = normal_values(splits[5], (CHANNELS,), 0.5, 2.5, (), jnp.float32)
    second_gain = jnp.clip(1.0 + 0.15 * jax.random.normal(splits[6], (CHANNELS,), jnp.float32), 0.25, 1.75)
    second_shift = normal_values(splits[7], (CHANNELS,), 0.3, 1.5, (), jnp.float32)
    temporal_bias = normal_values(splits[8], (CHANNELS,), 0.3, 1.5, (), jnp.float32)
    return dict(activations=activations, spatial_weight=spatial_weight, temporal_weight=temporal_weight, first_gain=first_gain, first_shift=first_shift, spatial_bias=spatial_bias, second_gain=second_gain, second_shift=second_shift, temporal_bias=temporal_bias)


EPS = 1e-05

def norm_silu(field, gain, shift):
    samples = field.shape[0]
    width = field.shape[-1] // GROUPS
    grouped = field.reshape(samples, -1, GROUPS, width)
    count = grouped.shape[1] * width
    sums = lax.optimization_barrier(jnp.sum(grouped, axis=(1, 3)))
    squares = lax.optimization_barrier(jnp.sum(grouped * grouped, axis=(1, 3)))
    mean = sums / count
    variance = squares / count - mean * mean
    inverse = lax.rsqrt(variance + EPS)
    mean_full = jnp.repeat(mean, width, axis=1)[:, None, None, None, :]
    inverse_full = jnp.repeat(inverse, width, axis=1)[:, None, None, None, :]
    normed = (field - mean_full) * inverse_full * gain + shift
    return jax.nn.silu(normed).astype(jnp.bfloat16)

def conv_taps(padded, weights, rows, cols):
    leading = padded.shape[0] * padded.shape[1]
    channels = padded.shape[-1]
    summed = jnp.zeros((leading * rows * cols, weights.shape[-1]), jnp.float32)
    for row_tap in range(3):
        for col_tap in range(3):
            section = padded[:, :, row_tap:row_tap + rows, col_tap:col_tap + cols, :].reshape(-1, channels)
            summed = summed + jnp.dot(section, weights[3 * row_tap + col_tap], preferred_element_type=jnp.float32)
    return summed.reshape(padded.shape[0], padded.shape[1], rows, cols, -1)

def reference(activations, spatial_weight, temporal_weight, first_gain, first_shift, spatial_bias, second_gain, second_shift, temporal_bias):
    inputs = activations.astype(jnp.float32)
    first = norm_silu(inputs, first_gain, first_shift)

    def spatial_one(frames):
        padded = jnp.pad(frames[None], ((0, 0), (0, 0), (1, 1), (1, 1), (0, 0)))
        return conv_taps(padded, spatial_weight, ROWS, COLS)[0]
    spatial = lax.map(spatial_one, first) + spatial_bias
    second = norm_silu(spatial, second_gain, second_shift)

    def temporal_one(frames):
        padded = jnp.pad(frames, ((1, 1), (0, 0), (0, 0), (0, 0)))
        summed = jnp.zeros((FRAMES * ROWS * COLS, CHANNELS), jnp.float32)
        for tap in range(3):
            section = padded[tap:tap + FRAMES].reshape(-1, CHANNELS)
            summed = summed + jnp.dot(section, temporal_weight[tap], preferred_element_type=jnp.float32)
        return summed.reshape(FRAMES, ROWS, COLS, CHANNELS)
    temporal = lax.map(temporal_one, second)
    return inputs + temporal + temporal_bias
```

```python
import numpy as np

import jax
import jax.numpy as jnp
from jax import lax
from jax.sharding import PartitionSpec as P

GROUPS = 32


EPS = 1e-05


def pair_sum(value, axis):
    if lax.axis_size(axis) == 2:
        return jax.tree.map(
            lambda v: v + lax.ppermute(v, axis, [(0, 1), (1, 0)]), value
        )
    return lax.psum(value, axis)


def gather_rep(w):
    size = lax.axis_size("rep")
    if size & (size - 1) != 0:
        return lax.all_gather(w, "rep", axis=w.ndim - 1, tiled=True), list(range(size))
    index = lax.axis_index("rep")
    blocks = w[None]
    order = [0]
    step = size // 2
    while step >= 1:
        recv = lax.ppermute(blocks, "rep", [(k, k ^ step) for k in range(size)])
        upper = (index & step) != 0
        low = jnp.where(upper, recv, blocks)
        high = jnp.where(upper, blocks, recv)
        blocks = jnp.concatenate([low, high], axis=0)
        order = order + [o + step for o in order]
        step //= 2
    out = jnp.moveaxis(blocks, 0, -2)
    return out.reshape(out.shape[:-2] + (-1,)), order


def local_vector(vec, order, frame_index, rep_size, frame_size):
    width = vec.shape[0] // (rep_size * frame_size)
    table = vec.reshape(rep_size, frame_size, width)[np.array(order)]
    return lax.dynamic_index_in_dim(table, frame_index, axis=1, keepdims=False).reshape(-1)


def silu_bf16(normed):
    return jax.nn.silu(normed).astype(jnp.bfloat16)


def shards(
    activations,
    spatial_weight,
    temporal_weight,
    first_gain,
    first_shift,
    spatial_bias,
    second_gain,
    second_shift,
    temporal_bias,
):
    rep_size = lax.axis_size("rep")
    frame_size = lax.axis_size("frame")
    row_size = lax.axis_size("row")
    frame_index = lax.axis_index("frame")
    row_index = lax.axis_index("row")
    channels = activations.shape[-1]
    rows = activations.shape[2]
    cols = activations.shape[3]
    width = channels // GROUPS
    shard_width = spatial_weight.shape[-1]

    spatial_w, order = gather_rep(spatial_weight)
    temporal_w, _ = gather_rep(temporal_weight)
    local = spatial_w.shape[-1]

    raw = lax.all_gather(activations, "frame", axis=1, tiled=True)
    frames = raw.shape[1]

    if row_size > 1:
        down = [(i, i + 1) for i in range(row_size - 1)]
        up = [(i + 1, i) for i in range(row_size - 1)]
        above = lax.ppermute(raw[:, :, rows - 1 :], "row", down)
        below = lax.ppermute(raw[:, :, :1], "row", up)
    else:
        above = jnp.zeros_like(raw[:, :, :1])
        below = jnp.zeros_like(raw[:, :, :1])

    inputs = raw.astype(jnp.float32)
    grouped = inputs.reshape(1, -1, GROUPS, width)
    sums = jnp.sum(grouped, axis=(1, 3))
    squares = jnp.sum(grouped * grouped, axis=(1, 3))
    sums, squares = pair_sum((sums, squares), "row")
    count = grouped.shape[1] * width * row_size
    mean = sums / count
    variance = squares / count - mean * mean
    inverse = lax.rsqrt(variance + EPS)
    mean_full = jnp.repeat(mean, width, axis=1)[:, None, None, None, :]
    inverse_full = jnp.repeat(inverse, width, axis=1)[:, None, None, None, :]

    def first_norm(x):
        normed = (x.astype(jnp.float32) - mean_full) * inverse_full * first_gain + first_shift
        return silu_bf16(normed)

    first_mid = first_norm(raw)
    first_above = jnp.where(row_index > 0, first_norm(above), jnp.zeros((), jnp.bfloat16))
    first_below = jnp.where(
        row_index < row_size - 1, first_norm(below), jnp.zeros((), jnp.bfloat16)
    )
    padded = jnp.concatenate([first_above, first_mid, first_below], axis=2)

    lhs = padded.reshape(frames, rows + 2, cols, channels)
    kernel = spatial_w.reshape(3, 3, channels, local)
    spatial = lax.conv_general_dilated(
        lhs,
        kernel,
        window_strides=(1, 1),
        padding=((0, 0), (1, 1)),
        dimension_numbers=("NHWC", "HWIO", "NHWC"),
        preferred_element_type=jnp.float32,
    )
    spatial = spatial + local_vector(spatial_bias, order, frame_index, rep_size, frame_size)

    g2 = local_vector(second_gain, order, frame_index, rep_size, frame_size)
    s2 = local_vector(second_shift, order, frame_index, rep_size, frame_size)
    if shard_width % width == 0:
        grouped2 = spatial.reshape(-1, local // width, width)
        sums2 = jnp.sum(grouped2, axis=(0, 2))
        squares2 = jnp.sum(grouped2 * grouped2, axis=(0, 2))
        sums2, squares2 = pair_sum((sums2, squares2), "row")
        count2 = grouped2.shape[0] * width * row_size
        mean2 = sums2 / count2
        variance2 = squares2 / count2 - mean2 * mean2
        inverse2 = lax.rsqrt(variance2 + EPS)
        mean2_full = jnp.repeat(mean2, width)
        inverse2_full = jnp.repeat(inverse2, width)
    else:
        flat = spatial.reshape(-1, local)
        csum = jnp.sum(flat, axis=0)
        csq = jnp.sum(flat * flat, axis=0)
        csum, csq = pair_sum((csum, csq), "row")
        both = lax.all_gather(jnp.stack([csum, csq]), "frame", axis=0)
        both = both.reshape(frame_size, 2, rep_size, shard_width)
        inv_order = np.argsort(np.array(order))
        both = both[:, :, inv_order]
        both = jnp.transpose(both, (1, 2, 0, 3)).reshape(2, GROUPS, -1)
        gsum = jnp.sum(both, axis=2)
        count2 = flat.shape[0] * row_size * width
        gmean = gsum[0] / count2
        gvar = gsum[1] / count2 - gmean * gmean
        ginv = lax.rsqrt(gvar + EPS)
        mean2_full = local_vector(jnp.repeat(gmean, width), order, frame_index, rep_size, frame_size)
        inverse2_full = local_vector(jnp.repeat(ginv, width), order, frame_index, rep_size, frame_size)
    second = silu_bf16((spatial - mean2_full) * inverse2_full * g2 + s2)

    second_all = lax.all_gather(second, "frame", axis=3, tiled=True)
    rows_order = np.arange(channels).reshape(rep_size, frame_size, shard_width)
    rows_order = rows_order[np.array(order)].transpose(1, 0, 2).reshape(-1)
    temporal_w = temporal_w[:, rows_order, :]
    lhs_t = second_all.reshape(frames, rows * cols, frame_size * local)[None]
    kernel_t = temporal_w.reshape(3, 1, frame_size * local, local)
    temporal = lax.conv_general_dilated(
        lhs_t,
        kernel_t,
        window_strides=(1, 1),
        padding=((1, 1), (0, 0)),
        dimension_numbers=("NHWC", "HWIO", "NHWC"),
        preferred_element_type=jnp.float32,
    )
    temporal = temporal.reshape(1, frames, rows, cols, local).astype(jnp.bfloat16)
    back = lax.all_to_all(temporal, "frame", split_axis=1, concat_axis=4, tiled=True)
    per_frame = frames // frame_size
    back = back.reshape(1, per_frame, rows, cols, frame_size, rep_size, shard_width)
    back = back[:, :, :, :, :, np.argsort(np.array(order))]
    back = jnp.swapaxes(back, 4, 5).reshape(1, per_frame, rows, cols, channels)
    return activations.astype(jnp.float32) + back.astype(jnp.float32) + temporal_bias


def solution(mesh):
    placed = (
        P("rep", "frame", "row", None, None),
        P(None, None, ("rep", "frame")),
        P(None, None, ("rep", "frame")),
        P(),
        P(),
        P(),
        P(),
        P(),
        P(),
    )
    return jax.shard_map(
        shards,
        mesh=mesh,
        in_specs=placed,
        out_specs=P("rep", "frame", "row", None, None),
        check_vma=False,
    )
```

```python
import numpy as np

import jax
import jax.numpy as jnp
from jax import lax
from jax.sharding import PartitionSpec as P

GROUPS = 32


EPS = 1e-05


def pair_sum(value, axis):
    if lax.axis_size(axis) == 2:
        return jax.tree.map(
            lambda v: v + lax.ppermute(v, axis, [(0, 1), (1, 0)]), value
        )
    return lax.psum(value, axis)


def gather_rep(w):
    size = lax.axis_size("rep")
    if size != 4:
        return lax.all_gather(w, "rep", axis=w.ndim - 1, tiled=True)
    index = lax.axis_index("rep")
    across = lax.ppermute(w, "rep", [(k, k ^ 2) for k in range(size)])
    partner = lax.ppermute(w, "rep", [(k, k ^ 1) for k in range(size)])
    diagonal = lax.ppermute(across, "rep", [(k, k ^ 1) for k in range(size)])
    held = [w, partner, across, diagonal]
    blocks = []
    for position in range(size):
        offset = index ^ position
        block = held[3]
        for d in (2, 1, 0):
            block = jnp.where(offset == d, held[d], block)
        blocks.append(block)
    return jnp.concatenate(blocks, axis=-1)


def local_vector(vec, frame_index, rep_size, frame_size):
    width = vec.shape[0] // (rep_size * frame_size)
    table = vec.reshape(rep_size, frame_size, width)
    return lax.dynamic_index_in_dim(table, frame_index, axis=1, keepdims=False).reshape(-1)


def silu_bf16(normed):
    return jax.nn.silu(normed).astype(jnp.bfloat16)


def temporal_wide(activations, second, temporal_w, temporal_bias):
    rep_size = lax.axis_size("rep")
    frame_size = lax.axis_size("frame")
    channels = activations.shape[-1]
    _, frames, rows, cols, local = second.shape
    shard_width = local // rep_size
    second_all = lax.all_gather(second, "frame", axis=4, tiled=True)
    rows_order = np.arange(channels).reshape(rep_size, frame_size, shard_width)
    rows_order = rows_order.transpose(1, 0, 2).reshape(-1)
    temporal_w = temporal_w[:, rows_order, :]
    lhs_t = second_all.reshape(frames, rows * cols, channels)[None]
    kernel_t = temporal_w.reshape(3, 1, channels, local)
    temporal = lax.conv_general_dilated(
        lhs_t,
        kernel_t,
        window_strides=(1, 1),
        padding=((1, 1), (0, 0)),
        dimension_numbers=("NHWC", "HWIO", "NHWC"),
        preferred_element_type=jnp.float32,
    )
    temporal = temporal.reshape(1, frames, rows, cols, local).astype(jnp.bfloat16)
    back = lax.all_to_all(temporal, "frame", split_axis=1, concat_axis=4, tiled=True)
    per_frame = frames // frame_size
    back = back.reshape(1, per_frame, rows, cols, frame_size, rep_size, shard_width)
    back = jnp.swapaxes(back, 4, 5).reshape(1, per_frame, rows, cols, channels)
    return activations.astype(jnp.float32) + back.astype(jnp.float32) + temporal_bias


def shards(
    activations,
    spatial_weight,
    temporal_weight,
    first_gain,
    first_shift,
    spatial_bias,
    second_gain,
    second_shift,
    temporal_bias,
):
    rep_size = lax.axis_size("rep")
    frame_size = lax.axis_size("frame")
    row_size = lax.axis_size("row")
    frame_index = lax.axis_index("frame")
    row_index = lax.axis_index("row")
    channels = activations.shape[-1]
    rows = activations.shape[2]
    cols = activations.shape[3]
    width = channels // GROUPS
    shard_width = spatial_weight.shape[-1]

    spatial_w = gather_rep(spatial_weight)
    temporal_w = gather_rep(temporal_weight)
    local = spatial_w.shape[-1]

    raw = lax.all_gather(activations, "frame", axis=1, tiled=True)
    frames = raw.shape[1]

    if row_size > 1:
        down = [(i, i + 1) for i in range(row_size - 1)]
        up = [(i + 1, i) for i in range(row_size - 1)]
        above = lax.ppermute(raw[:, :, rows - 1 :], "row", down)
        below = lax.ppermute(raw[:, :, :1], "row", up)
    else:
        above = jnp.zeros_like(raw[:, :, :1])
        below = jnp.zeros_like(raw[:, :, :1])

    inputs = raw.astype(jnp.float32)
    grouped = inputs.reshape(1, -1, GROUPS, width)
    sums = jnp.sum(grouped, axis=(1, 3))
    squares = jnp.sum(grouped * grouped, axis=(1, 3))
    sums, squares = pair_sum((sums, squares), "row")
    count = grouped.shape[1] * width * row_size
    mean = sums / count
    variance = squares / count - mean * mean
    inverse = lax.rsqrt(variance + EPS)
    mean_full = jnp.repeat(mean, width, axis=1)[:, None, None, None, :]
    inverse_full = jnp.repeat(inverse, width, axis=1)[:, None, None, None, :]

    def first_norm(x):
        normed = (x.astype(jnp.float32) - mean_full) * inverse_full * first_gain + first_shift
        return silu_bf16(normed)

    first_mid = first_norm(raw)
    first_above = jnp.where(row_index > 0, first_norm(above), jnp.zeros((), jnp.bfloat16))
    first_below = jnp.where(
        row_index < row_size - 1, first_norm(below), jnp.zeros((), jnp.bfloat16)
    )
    padded = jnp.concatenate([first_above, first_mid, first_below], axis=2)

    field = lax.optimization_barrier(padded[0])
    spatial = None
    for col_tap in range(3):
        product = None
        for row_tap in range(3):
            term = jnp.einsum(
                "frxc,cn->frxn",
                field[:, row_tap : row_tap + rows],
                spatial_w[3 * row_tap + col_tap],
                preferred_element_type=jnp.float32,
            )
            product = term if product is None else product + term
        if col_tap == 0:
            product = jnp.pad(product[:, :, :-1], ((0, 0), (0, 0), (1, 0), (0, 0)))
        elif col_tap == 2:
            product = jnp.pad(product[:, :, 1:], ((0, 0), (0, 0), (0, 1), (0, 0)))
        spatial = product if spatial is None else spatial + product
    spatial = spatial[None]
    spatial = spatial + local_vector(spatial_bias, frame_index, rep_size, frame_size)

    g2 = local_vector(second_gain, frame_index, rep_size, frame_size)
    s2 = local_vector(second_shift, frame_index, rep_size, frame_size)
    if shard_width % width == 0:
        grouped2 = spatial.reshape(-1, local // width, width)
        sums2 = jnp.sum(grouped2, axis=(0, 2))
        squares2 = jnp.sum(grouped2 * grouped2, axis=(0, 2))
        sums2, squares2 = pair_sum((sums2, squares2), "row")
        count2 = grouped2.shape[0] * width * row_size
        mean2 = sums2 / count2
        variance2 = squares2 / count2 - mean2 * mean2
        inverse2 = lax.rsqrt(variance2 + EPS)
        mean2_full = jnp.repeat(mean2, width)
        inverse2_full = jnp.repeat(inverse2, width)
    else:
        flat = spatial.reshape(-1, local)
        csum = jnp.sum(flat, axis=0)
        csq = jnp.sum(flat * flat, axis=0)
        csum, csq = pair_sum((csum, csq), "row")
        both = lax.all_gather(jnp.stack([csum, csq]), "frame", axis=0)
        both = both.reshape(frame_size, 2, rep_size, shard_width)
        both = jnp.transpose(both, (1, 2, 0, 3)).reshape(2, GROUPS, -1)
        gsum = jnp.sum(both, axis=2)
        count2 = flat.shape[0] * row_size * width
        gmean = gsum[0] / count2
        gvar = gsum[1] / count2 - gmean * gmean
        ginv = lax.rsqrt(gvar + EPS)
        mean2_full = local_vector(jnp.repeat(gmean, width), frame_index, rep_size, frame_size)
        inverse2_full = local_vector(jnp.repeat(ginv, width), frame_index, rep_size, frame_size)
    second = silu_bf16((spatial - mean2_full) * inverse2_full * g2 + s2)

    if frame_size > 8:
        return temporal_wide(activations, second, temporal_w, temporal_bias)
    second_all = lax.all_gather(second[0], "frame", axis=0, tiled=False)
    taps = temporal_w.reshape(3, rep_size, frame_size, shard_width, local)
    temporal = None
    for group in range(frame_size):
        block = second_all[group]
        weights = taps[:, :, group].reshape(3, rep_size * shard_width, local)
        for tap in range(3):
            if tap == 1:
                source = block
            elif tap == 0:
                source = block[:-1]
            else:
                source = block[1:]
            if source.shape[0] == 0:
                continue
            term = jnp.einsum(
                "frxc,cn->frxn", source, weights[tap], preferred_element_type=jnp.float32
            )
            if tap == 0:
                term = jnp.pad(term, ((1, 0), (0, 0), (0, 0), (0, 0)))
            elif tap == 2:
                term = jnp.pad(term, ((0, 1), (0, 0), (0, 0), (0, 0)))
            temporal = term if temporal is None else temporal + term
    temporal = temporal.astype(jnp.bfloat16)

    per_frame = frames // frame_size
    result = jnp.zeros((per_frame, rows, cols, rep_size, frame_size, shard_width), jnp.float32)
    for shift in range(frame_size):
        target = (frame_index + shift) % frame_size
        piece = lax.dynamic_slice_in_dim(temporal, target * per_frame, per_frame, axis=0)
        if shift:
            piece = lax.ppermute(
                piece, "frame", [(k, (k + shift) % frame_size) for k in range(frame_size)]
            )
        source = (frame_index - shift) % frame_size
        piece = piece.reshape(per_frame, rows, cols, rep_size, 1, shard_width)
        result = lax.dynamic_update_slice_in_dim(
            result, piece.astype(jnp.float32), source, axis=4
        )
    result = result.reshape(1, per_frame, rows, cols, channels)
    return activations.astype(jnp.float32) + result + temporal_bias


def solution(mesh):
    placed = (
        P("rep", "frame", "row", None, None),
        P(None, None, ("rep", "frame")),
        P(None, None, ("rep", "frame")),
        P(),
        P(),
        P(),
        P(),
        P(),
        P(),
    )
    return jax.shard_map(
        shards,
        mesh=mesh,
        in_specs=placed,
        out_specs=P("rep", "frame", "row", None, None),
        check_vma=False,
    )
```

```python
import numpy as np

import jax
import jax.numpy as jnp
from jax import lax
from jax.sharding import PartitionSpec as P


GROUPS = 32


EPS = 1e-05


def pair_sum(value, axis):
    if lax.axis_size(axis) == 2:
        return jax.tree.map(
            lambda v: v + lax.ppermute(v, axis, [(0, 1), (1, 0)]), value
        )
    return lax.psum(value, axis)


def gather_rep(w):
    size = lax.axis_size("rep")
    if size != 4:
        return lax.all_gather(w, "rep", axis=w.ndim - 1, tiled=True)
    index = lax.axis_index("rep")
    across = lax.ppermute(w, "rep", [(k, k ^ 2) for k in range(size)])
    partner = lax.ppermute(w, "rep", [(k, k ^ 1) for k in range(size)])
    diagonal = lax.ppermute(across, "rep", [(k, k ^ 1) for k in range(size)])
    held = [w, partner, across, diagonal]
    blocks = []
    for position in range(size):
        offset = index ^ position
        block = held[3]
        for d in (2, 1, 0):
            block = jnp.where(offset == d, held[d], block)
        blocks.append(block)
    return jnp.concatenate(blocks, axis=-1)


def local_vector(vec, frame_index, rep_size, frame_size):
    width = vec.shape[0] // (rep_size * frame_size)
    table = vec.reshape(rep_size, frame_size, width)
    return lax.dynamic_index_in_dim(table, frame_index, axis=1, keepdims=False).reshape(-1)


def silu_bf16(normed):
    return jax.nn.silu(normed).astype(jnp.bfloat16)


def temporal_wide(activations, second, temporal_w, temporal_bias):
    rep_size = lax.axis_size("rep")
    frame_size = lax.axis_size("frame")
    channels = activations.shape[-1]
    _, frames, rows, cols, local = second.shape
    shard_width = local // rep_size
    second_all = lax.all_gather(second, "frame", axis=4, tiled=True)
    rows_order = np.arange(channels).reshape(rep_size, frame_size, shard_width)
    rows_order = rows_order.transpose(1, 0, 2).reshape(-1)
    temporal_w = temporal_w[:, rows_order, :]
    lhs_t = second_all.reshape(frames, rows * cols, channels)[None]
    kernel_t = temporal_w.reshape(3, 1, channels, local)
    temporal = lax.conv_general_dilated(
        lhs_t,
        kernel_t,
        window_strides=(1, 1),
        padding=((1, 1), (0, 0)),
        dimension_numbers=("NHWC", "HWIO", "NHWC"),
        preferred_element_type=jnp.float32,
    )
    temporal = temporal.reshape(1, frames, rows, cols, local).astype(jnp.bfloat16)
    back = lax.all_to_all(temporal, "frame", split_axis=1, concat_axis=4, tiled=True)
    per_frame = frames // frame_size
    back = back.reshape(1, per_frame, rows, cols, frame_size, rep_size, shard_width)
    back = jnp.swapaxes(back, 4, 5).reshape(1, per_frame, rows, cols, channels)
    return activations.astype(jnp.float32) + back.astype(jnp.float32) + temporal_bias


def shards(
    activations,
    spatial_weight,
    temporal_weight,
    first_gain,
    first_shift,
    spatial_bias,
    second_gain,
    second_shift,
    temporal_bias,
):
    rep_size = lax.axis_size("rep")
    frame_size = lax.axis_size("frame")
    row_size = lax.axis_size("row")
    frame_index = lax.axis_index("frame")
    row_index = lax.axis_index("row")
    channels = activations.shape[-1]
    rows = activations.shape[2]
    cols = activations.shape[3]
    width = channels // GROUPS
    shard_width = spatial_weight.shape[-1]

    spatial_w = gather_rep(spatial_weight)
    temporal_w = gather_rep(temporal_weight)
    local = spatial_w.shape[-1]

    raw = lax.all_gather(activations, "frame", axis=1, tiled=True)
    frames = raw.shape[1]

    if row_size > 1:
        down = [(i, i + 1) for i in range(row_size - 1)]
        up = [(i + 1, i) for i in range(row_size - 1)]
        above = lax.ppermute(raw[:, :, rows - 1 :], "row", down)
        below = lax.ppermute(raw[:, :, :1], "row", up)
    else:
        above = jnp.zeros_like(raw[:, :, :1])
        below = jnp.zeros_like(raw[:, :, :1])

    inputs = raw.astype(jnp.float32)
    grouped = inputs.reshape(1, -1, GROUPS, width)
    sums = jnp.sum(grouped, axis=(1, 3))
    squares = jnp.sum(grouped * grouped, axis=(1, 3))
    sums, squares = pair_sum((sums, squares), "row")
    count = grouped.shape[1] * width * row_size
    mean = sums / count
    variance = squares / count - mean * mean
    inverse = lax.rsqrt(variance + EPS)
    mean_full = jnp.repeat(mean, width, axis=1)[:, None, None, None, :]
    inverse_full = jnp.repeat(inverse, width, axis=1)[:, None, None, None, :]

    def first_norm(x):
        normed = (x.astype(jnp.float32) - mean_full) * inverse_full * first_gain + first_shift
        return silu_bf16(normed)

    first_mid = first_norm(raw)
    first_above = jnp.where(row_index > 0, first_norm(above), jnp.zeros((), jnp.bfloat16))
    first_below = jnp.where(
        row_index < row_size - 1, first_norm(below), jnp.zeros((), jnp.bfloat16)
    )
    padded = jnp.concatenate([first_above, first_mid, first_below], axis=2)

    field = lax.optimization_barrier(padded[0])
    spatial = None
    for col_tap in range(3):
        product = None
        for row_tap in range(3):
            term = jnp.einsum(
                "frxc,cn->frxn",
                field[:, row_tap : row_tap + rows],
                spatial_w[3 * row_tap + col_tap],
                preferred_element_type=jnp.float32,
            )
            product = term if product is None else product + term
        if col_tap == 0:
            product = jnp.pad(product[:, :, :-1], ((0, 0), (0, 0), (1, 0), (0, 0)))
        elif col_tap == 2:
            product = jnp.pad(product[:, :, 1:], ((0, 0), (0, 0), (0, 1), (0, 0)))
        spatial = product if spatial is None else spatial + product
    spatial = spatial[None]
    spatial = spatial + local_vector(spatial_bias, frame_index, rep_size, frame_size)

    g2 = local_vector(second_gain, frame_index, rep_size, frame_size)
    s2 = local_vector(second_shift, frame_index, rep_size, frame_size)
    if shard_width % width == 0:
        grouped2 = spatial.reshape(-1, local // width, width)
        sums2 = jnp.sum(grouped2, axis=(0, 2))
        squares2 = jnp.sum(grouped2 * grouped2, axis=(0, 2))
        sums2, squares2 = pair_sum((sums2, squares2), "row")
        count2 = grouped2.shape[0] * width * row_size
        mean2 = sums2 / count2
        variance2 = squares2 / count2 - mean2 * mean2
        inverse2 = lax.rsqrt(variance2 + EPS)
        mean2_full = jnp.repeat(mean2, width)
        inverse2_full = jnp.repeat(inverse2, width)
    else:
        flat = spatial.reshape(-1, local)
        csum = jnp.sum(flat, axis=0)
        csq = jnp.sum(flat * flat, axis=0)
        csum, csq = pair_sum((csum, csq), "row")
        both = lax.all_gather(jnp.stack([csum, csq]), "frame", axis=0)
        both = both.reshape(frame_size, 2, rep_size, shard_width)
        both = jnp.transpose(both, (1, 2, 0, 3)).reshape(2, GROUPS, -1)
        gsum = jnp.sum(both, axis=2)
        count2 = flat.shape[0] * row_size * width
        gmean = gsum[0] / count2
        gvar = gsum[1] / count2 - gmean * gmean
        ginv = lax.rsqrt(gvar + EPS)
        mean2_full = local_vector(jnp.repeat(gmean, width), frame_index, rep_size, frame_size)
        inverse2_full = local_vector(jnp.repeat(ginv, width), frame_index, rep_size, frame_size)
    second = silu_bf16((spatial - mean2_full) * inverse2_full * g2 + s2)

    if frame_size > 8:
        return temporal_wide(activations, second, temporal_w, temporal_bias)
    second_all = lax.all_gather(second[0], "frame", axis=0, tiled=False)
    taps = temporal_w.reshape(3, rep_size, frame_size, shard_width, local)
    temporal = None
    for group in range(frame_size):
        block = second_all[group]
        weights = taps[:, :, group].reshape(3, rep_size * shard_width, local)
        for tap in range(3):
            if tap == 1:
                source = block
            elif tap == 0:
                source = block[:-1]
            else:
                source = block[1:]
            if source.shape[0] == 0:
                continue
            term = jnp.einsum(
                "frxc,cn->frxn", source, weights[tap], preferred_element_type=jnp.float32
            )
            if tap == 0:
                term = jnp.pad(term, ((1, 0), (0, 0), (0, 0), (0, 0)))
            elif tap == 2:
                term = jnp.pad(term, ((0, 1), (0, 0), (0, 0), (0, 0)))
            temporal = term if temporal is None else temporal + term
    temporal = temporal.astype(jnp.bfloat16)

    per_frame = frames // frame_size
    pieces = []
    for shift in range(frame_size):
        target = (frame_index + shift) % frame_size
        piece = lax.dynamic_slice_in_dim(temporal, target * per_frame, per_frame, axis=0)
        if shift:
            piece = lax.ppermute(
                piece, "frame", [(k, (k + shift) % frame_size) for k in range(frame_size)]
            )
        pieces.append(piece.reshape(per_frame, rows, cols, rep_size, shard_width))
    slots = []
    for group in range(frame_size):
        wanted = (frame_index - group) % frame_size
        slot = pieces[frame_size - 1]
        for shift in range(frame_size - 2, -1, -1):
            slot = jnp.where(wanted == shift, pieces[shift], slot)
        slots.append(slot)
    result = jnp.stack(slots, axis=4).reshape(1, per_frame, rows, cols, channels)
    return activations.astype(jnp.float32) + result.astype(jnp.float32) + temporal_bias


def solution(mesh):
    placed = (
        P("rep", "frame", "row", None, None),
        P(None, None, ("rep", "frame")),
        P(None, None, ("rep", "frame")),
        P(),
        P(),
        P(),
        P(),
        P(),
        P(),
    )

    return jax.shard_map(
        shards,
        mesh=mesh,
        in_specs=placed,
        out_specs=P("rep", "frame", "row", None, None),
        check_vma=False,
    )
```

```python
import numpy as np

import jax
import jax.numpy as jnp
from jax import lax
from jax.sharding import PartitionSpec as P


GROUPS = 32


EPS = 1e-05


def pair_sum(value, axis):
    if lax.axis_size(axis) == 2:
        return jax.tree.map(
            lambda v: v + lax.ppermute(v, axis, [(0, 1), (1, 0)]), value
        )
    return lax.psum(value, axis)


def gather_rep(w):
    size = lax.axis_size("rep")
    if size != 4:
        return lax.all_gather(w, "rep", axis=w.ndim - 1, tiled=True)
    index = lax.axis_index("rep")
    across = lax.ppermute(w, "rep", [(k, k ^ 2) for k in range(size)])
    partner = lax.ppermute(w, "rep", [(k, k ^ 1) for k in range(size)])
    diagonal = lax.ppermute(across, "rep", [(k, k ^ 1) for k in range(size)])
    held = [w, partner, across, diagonal]
    blocks = []
    for position in range(size):
        offset = index ^ position
        block = held[3]
        for d in (2, 1, 0):
            block = jnp.where(offset == d, held[d], block)
        blocks.append(block)
    return jnp.concatenate(blocks, axis=-1)


def local_vector(vec, frame_index, rep_size, frame_size):
    width = vec.shape[0] // (rep_size * frame_size)
    table = vec.reshape(rep_size, frame_size, width)
    return lax.dynamic_index_in_dim(table, frame_index, axis=1, keepdims=False).reshape(-1)


def silu_bf16(normed):
    return jax.nn.silu(normed).astype(jnp.bfloat16)


def temporal_wide(activations, second, temporal_w, temporal_bias):
    rep_size = lax.axis_size("rep")
    frame_size = lax.axis_size("frame")
    channels = activations.shape[-1]
    _, frames, rows, cols, local = second.shape
    shard_width = local // rep_size
    second_all = lax.all_gather(second, "frame", axis=4, tiled=True)
    rows_order = np.arange(channels).reshape(rep_size, frame_size, shard_width)
    rows_order = rows_order.transpose(1, 0, 2).reshape(-1)
    temporal_w = temporal_w[:, rows_order, :]
    lhs_t = second_all.reshape(frames, rows * cols, channels)[None]
    kernel_t = temporal_w.reshape(3, 1, channels, local)
    temporal = lax.conv_general_dilated(
        lhs_t,
        kernel_t,
        window_strides=(1, 1),
        padding=((1, 1), (0, 0)),
        dimension_numbers=("NHWC", "HWIO", "NHWC"),
        preferred_element_type=jnp.float32,
    )
    temporal = temporal.reshape(1, frames, rows, cols, local).astype(jnp.bfloat16)
    back = lax.all_to_all(temporal, "frame", split_axis=1, concat_axis=4, tiled=True)
    per_frame = frames // frame_size
    back = back.reshape(1, per_frame, rows, cols, frame_size, rep_size, shard_width)
    back = jnp.swapaxes(back, 4, 5).reshape(1, per_frame, rows, cols, channels)
    return activations.astype(jnp.float32) + back.astype(jnp.float32) + temporal_bias


def spatial_part(field, weights, rows):
    out = None
    for col_tap in range(3):
        product = None
        for row_tap in range(3):
            term = jnp.einsum(
                "frxc,cn->frxn",
                field[:, row_tap : row_tap + rows],
                weights[3 * row_tap + col_tap],
                preferred_element_type=jnp.float32,
            )
            product = term if product is None else product + term
        if col_tap == 0:
            product = jnp.pad(product[:, :, :-1], ((0, 0), (0, 0), (1, 0), (0, 0)))
        elif col_tap == 2:
            product = jnp.pad(product[:, :, 1:], ((0, 0), (0, 0), (0, 1), (0, 0)))
        out = product if out is None else out + product
    return out


def group_norm_part(field, width, spread):
    grouped = field.reshape(-1, field.shape[-1] // width, width)
    sums = jnp.sum(grouped, axis=(0, 2))
    squares = jnp.sum(grouped * grouped, axis=(0, 2))
    sums, squares = pair_sum((sums, squares), "row")
    count = grouped.shape[0] * width * spread
    mean = sums / count
    variance = squares / count - mean * mean
    inverse = lax.rsqrt(variance + EPS)
    return jnp.repeat(mean, width), jnp.repeat(inverse, width)


def first_field(raw, gain, shift, width):
    row_size = lax.axis_size("row")
    row_index = lax.axis_index("row")
    rows = raw.shape[2]
    if row_size > 1:
        down = [(i, i + 1) for i in range(row_size - 1)]
        up = [(i + 1, i) for i in range(row_size - 1)]
        above = lax.ppermute(raw[:, :, rows - 1 :], "row", down)
        below = lax.ppermute(raw[:, :, :1], "row", up)
    else:
        above = jnp.zeros_like(raw[:, :, :1])
        below = jnp.zeros_like(raw[:, :, :1])
    mean, inverse = group_norm_part(raw.astype(jnp.float32), width, row_size)

    def norm(x):
        return silu_bf16((x.astype(jnp.float32) - mean) * inverse * gain + shift)

    first_above = jnp.where(row_index > 0, norm(above), jnp.zeros((), jnp.bfloat16))
    first_below = jnp.where(row_index < row_size - 1, norm(below), jnp.zeros((), jnp.bfloat16))
    padded = jnp.concatenate([first_above, norm(raw), first_below], axis=2)
    return lax.optimization_barrier(padded[0])


def pipelined(
    activations, spatial_w, temporal_w, first_gain, first_shift,
    spatial_bias, second_gain, second_shift, temporal_bias,
):
    rep_size = lax.axis_size("rep")
    frame_size = lax.axis_size("frame")
    row_size = lax.axis_size("row")
    frame_index = lax.axis_index("frame")
    channels = activations.shape[-1]
    rows = activations.shape[2]
    width = channels // GROUPS
    local = spatial_w.shape[-1]
    shard_width = local // rep_size
    part = channels // 2
    half = local // 2

    raws = [
        lax.all_gather(activations[..., h * part : (h + 1) * part], "frame", axis=1, tiled=True)
        for h in range(2)
    ]

    field = first_field(raws[0], first_gain[:part], first_shift[:part], width)
    partial = spatial_part(field, spatial_w[:, :part], rows)
    field = first_field(raws[1], first_gain[part:], first_shift[part:], width)
    bias = local_vector(spatial_bias, frame_index, rep_size, frame_size)
    g2 = local_vector(second_gain, frame_index, rep_size, frame_size)
    s2 = local_vector(second_shift, frame_index, rep_size, frame_size)
    gathered = []
    for h in range(2):
        span = slice(h * half, (h + 1) * half)
        spatial = partial[..., span] + spatial_part(field, spatial_w[:, part:, span], rows)
        spatial = spatial + bias[span]
        mean2, inverse2 = group_norm_part(spatial, width, row_size)
        second = silu_bf16((spatial - mean2) * inverse2 * g2[span] + s2[span])
        gathered.append(lax.all_gather(second, "frame", axis=0, tiled=False))

    taps = temporal_w.reshape(3, rep_size, frame_size, shard_width, local)
    temporal = None
    for h in range(2):
        blocks = slice(h * rep_size // 2, (h + 1) * rep_size // 2)
        for group in range(frame_size):
            block = gathered[h][group]
            weights = taps[:, blocks, group].reshape(3, half, local)
            for tap in range(3):
                if tap == 1:
                    source = block
                elif tap == 0:
                    source = block[:-1]
                else:
                    source = block[1:]
                if source.shape[0] == 0:
                    continue
                term = jnp.einsum(
                    "frxc,cn->frxn", source, weights[tap], preferred_element_type=jnp.float32
                )
                if tap == 0:
                    term = jnp.pad(term, ((1, 0), (0, 0), (0, 0), (0, 0)))
                elif tap == 2:
                    term = jnp.pad(term, ((0, 1), (0, 0), (0, 0), (0, 0)))
                temporal = term if temporal is None else temporal + term
    temporal = temporal.astype(jnp.bfloat16)
    return redistribute(activations, temporal, temporal_bias)


def redistribute(activations, temporal, temporal_bias):
    rep_size = lax.axis_size("rep")
    frame_size = lax.axis_size("frame")
    frame_index = lax.axis_index("frame")
    channels = activations.shape[-1]
    frames, rows, cols, local = temporal.shape
    shard_width = local // rep_size
    per_frame = frames // frame_size
    pieces = []
    for shift in range(frame_size):
        target = (frame_index + shift) % frame_size
        piece = lax.dynamic_slice_in_dim(temporal, target * per_frame, per_frame, axis=0)
        if shift:
            piece = lax.ppermute(
                piece, "frame", [(k, (k + shift) % frame_size) for k in range(frame_size)]
            )
        pieces.append(piece.reshape(per_frame, rows, cols, rep_size, shard_width))
    slots = []
    for group in range(frame_size):
        wanted = (frame_index - group) % frame_size
        slot = pieces[frame_size - 1]
        for shift in range(frame_size - 2, -1, -1):
            slot = jnp.where(wanted == shift, pieces[shift], slot)
        slots.append(slot)
    result = jnp.stack(slots, axis=4).reshape(1, per_frame, rows, cols, channels)
    return activations.astype(jnp.float32) + result.astype(jnp.float32) + temporal_bias


def shards(
    activations,
    spatial_weight,
    temporal_weight,
    first_gain,
    first_shift,
    spatial_bias,
    second_gain,
    second_shift,
    temporal_bias,
):
    rep_size = lax.axis_size("rep")
    frame_size = lax.axis_size("frame")
    row_size = lax.axis_size("row")
    frame_index = lax.axis_index("frame")
    row_index = lax.axis_index("row")
    channels = activations.shape[-1]
    rows = activations.shape[2]
    width = channels // GROUPS
    shard_width = spatial_weight.shape[-1]

    spatial_w = gather_rep(spatial_weight)
    temporal_w = gather_rep(temporal_weight)
    local = spatial_w.shape[-1]

    if frame_size <= 8 and rep_size % 2 == 0 and shard_width % width == 0:
        return pipelined(
            activations, spatial_w, temporal_w, first_gain, first_shift,
            spatial_bias, second_gain, second_shift, temporal_bias,
        )
    raw = lax.all_gather(activations, "frame", axis=1, tiled=True)

    if row_size > 1:
        down = [(i, i + 1) for i in range(row_size - 1)]
        up = [(i + 1, i) for i in range(row_size - 1)]
        above = lax.ppermute(raw[:, :, rows - 1 :], "row", down)
        below = lax.ppermute(raw[:, :, :1], "row", up)
    else:
        above = jnp.zeros_like(raw[:, :, :1])
        below = jnp.zeros_like(raw[:, :, :1])

    inputs = raw.astype(jnp.float32)
    grouped = inputs.reshape(1, -1, GROUPS, width)
    sums = jnp.sum(grouped, axis=(1, 3))
    squares = jnp.sum(grouped * grouped, axis=(1, 3))
    sums, squares = pair_sum((sums, squares), "row")
    count = grouped.shape[1] * width * row_size
    mean = sums / count
    variance = squares / count - mean * mean
    inverse = lax.rsqrt(variance + EPS)
    mean_full = jnp.repeat(mean, width, axis=1)[:, None, None, None, :]
    inverse_full = jnp.repeat(inverse, width, axis=1)[:, None, None, None, :]

    def first_norm(x):
        normed = (x.astype(jnp.float32) - mean_full) * inverse_full * first_gain + first_shift
        return silu_bf16(normed)

    first_mid = first_norm(raw)
    first_above = jnp.where(row_index > 0, first_norm(above), jnp.zeros((), jnp.bfloat16))
    first_below = jnp.where(
        row_index < row_size - 1, first_norm(below), jnp.zeros((), jnp.bfloat16)
    )
    padded = jnp.concatenate([first_above, first_mid, first_below], axis=2)

    field = lax.optimization_barrier(padded[0])
    spatial = None
    for col_tap in range(3):
        product = None
        for row_tap in range(3):
            term = jnp.einsum(
                "frxc,cn->frxn",
                field[:, row_tap : row_tap + rows],
                spatial_w[3 * row_tap + col_tap],
                preferred_element_type=jnp.float32,
            )
            product = term if product is None else product + term
        if col_tap == 0:
            product = jnp.pad(product[:, :, :-1], ((0, 0), (0, 0), (1, 0), (0, 0)))
        elif col_tap == 2:
            product = jnp.pad(product[:, :, 1:], ((0, 0), (0, 0), (0, 1), (0, 0)))
        spatial = product if spatial is None else spatial + product
    spatial = spatial[None]
    spatial = spatial + local_vector(spatial_bias, frame_index, rep_size, frame_size)

    g2 = local_vector(second_gain, frame_index, rep_size, frame_size)
    s2 = local_vector(second_shift, frame_index, rep_size, frame_size)
    if shard_width % width == 0:
        grouped2 = spatial.reshape(-1, local // width, width)
        sums2 = jnp.sum(grouped2, axis=(0, 2))
        squares2 = jnp.sum(grouped2 * grouped2, axis=(0, 2))
        sums2, squares2 = pair_sum((sums2, squares2), "row")
        count2 = grouped2.shape[0] * width * row_size
        mean2 = sums2 / count2
        variance2 = squares2 / count2 - mean2 * mean2
        inverse2 = lax.rsqrt(variance2 + EPS)
        mean2_full = jnp.repeat(mean2, width)
        inverse2_full = jnp.repeat(inverse2, width)
    else:
        flat = spatial.reshape(-1, local)
        csum = jnp.sum(flat, axis=0)
        csq = jnp.sum(flat * flat, axis=0)
        csum, csq = pair_sum((csum, csq), "row")
        both = lax.all_gather(jnp.stack([csum, csq]), "frame", axis=0)
        both = both.reshape(frame_size, 2, rep_size, shard_width)
        both = jnp.transpose(both, (1, 2, 0, 3)).reshape(2, GROUPS, -1)
        gsum = jnp.sum(both, axis=2)
        count2 = flat.shape[0] * row_size * width
        gmean = gsum[0] / count2
        gvar = gsum[1] / count2 - gmean * gmean
        ginv = lax.rsqrt(gvar + EPS)
        mean2_full = local_vector(jnp.repeat(gmean, width), frame_index, rep_size, frame_size)
        inverse2_full = local_vector(jnp.repeat(ginv, width), frame_index, rep_size, frame_size)
    second = silu_bf16((spatial - mean2_full) * inverse2_full * g2 + s2)

    if frame_size > 8:
        return temporal_wide(activations, second, temporal_w, temporal_bias)
    second_all = lax.all_gather(second[0], "frame", axis=0, tiled=False)
    taps = temporal_w.reshape(3, rep_size, frame_size, shard_width, local)
    temporal = None
    for group in range(frame_size):
        block = second_all[group]
        weights = taps[:, :, group].reshape(3, rep_size * shard_width, local)
        for tap in range(3):
            if tap == 1:
                source = block
            elif tap == 0:
                source = block[:-1]
            else:
                source = block[1:]
            if source.shape[0] == 0:
                continue
            term = jnp.einsum(
                "frxc,cn->frxn", source, weights[tap], preferred_element_type=jnp.float32
            )
            if tap == 0:
                term = jnp.pad(term, ((1, 0), (0, 0), (0, 0), (0, 0)))
            elif tap == 2:
                term = jnp.pad(term, ((0, 1), (0, 0), (0, 0), (0, 0)))
            temporal = term if temporal is None else temporal + term
    temporal = temporal.astype(jnp.bfloat16)

    return redistribute(activations, temporal, temporal_bias)


def solution(mesh):
    placed = (
        P("rep", "frame", "row", None, None),
        P(None, None, ("rep", "frame")),
        P(None, None, ("rep", "frame")),
        P(),
        P(),
        P(),
        P(),
        P(),
        P(),
    )

    return jax.shard_map(
        shards,
        mesh=mesh,
        in_specs=placed,
        out_specs=P("rep", "frame", "row", None, None),
        check_vma=False,
    )
```

```python
import numpy as np

import jax
import jax.numpy as jnp
from jax import lax
from jax.sharding import PartitionSpec as P


GROUPS = 32


EPS = 1e-05


def pair_sum(value, axis):
    if lax.axis_size(axis) == 2:
        return jax.tree.map(
            lambda v: v + lax.ppermute(v, axis, [(0, 1), (1, 0)]), value
        )
    return lax.psum(value, axis)


def butterfly_sum(value, axis):
    size = lax.axis_size(axis)
    if size & (size - 1) != 0:
        return lax.psum(value, axis)
    step = 1
    while step < size:
        pairs = [(k, k ^ step) for k in range(size)]
        value = jax.tree.map(lambda v: v + lax.ppermute(v, axis, pairs), value)
        step *= 2
    return value


def gather_rep(w):
    size = lax.axis_size("rep")
    if size != 4:
        return lax.all_gather(w, "rep", axis=w.ndim - 1, tiled=True)
    index = lax.axis_index("rep")
    across = lax.ppermute(w, "rep", [(k, k ^ 2) for k in range(size)])
    partner = lax.ppermute(w, "rep", [(k, k ^ 1) for k in range(size)])
    diagonal = lax.ppermute(across, "rep", [(k, k ^ 1) for k in range(size)])
    held = [w, partner, across, diagonal]
    blocks = []
    for position in range(size):
        offset = index ^ position
        block = held[3]
        for d in (2, 1, 0):
            block = jnp.where(offset == d, held[d], block)
        blocks.append(block)
    return jnp.concatenate(blocks, axis=-1)


def local_vector(vec, frame_index, rep_size, frame_size):
    width = vec.shape[0] // (rep_size * frame_size)
    table = vec.reshape(rep_size, frame_size, width)
    return lax.dynamic_index_in_dim(table, frame_index, axis=1, keepdims=False).reshape(-1)


def silu_bf16(normed):
    return jax.nn.silu(normed).astype(jnp.bfloat16)


def temporal_wide(activations, second, temporal_w, temporal_bias):
    rep_size = lax.axis_size("rep")
    frame_size = lax.axis_size("frame")
    channels = activations.shape[-1]
    _, frames, rows, cols, local = second.shape
    shard_width = local // rep_size
    second_all = lax.all_gather(second, "frame", axis=4, tiled=True)
    rows_order = np.arange(channels).reshape(rep_size, frame_size, shard_width)
    rows_order = rows_order.transpose(1, 0, 2).reshape(-1)
    temporal_w = temporal_w[:, rows_order, :]
    lhs_t = second_all.reshape(frames, rows * cols, channels)[None]
    kernel_t = temporal_w.reshape(3, 1, channels, local)
    temporal = lax.conv_general_dilated(
        lhs_t,
        kernel_t,
        window_strides=(1, 1),
        padding=((1, 1), (0, 0)),
        dimension_numbers=("NHWC", "HWIO", "NHWC"),
        preferred_element_type=jnp.float32,
    )
    temporal = temporal.reshape(1, frames, rows, cols, local).astype(jnp.bfloat16)
    back = lax.all_to_all(temporal, "frame", split_axis=1, concat_axis=4, tiled=True)
    per_frame = frames // frame_size
    back = back.reshape(1, per_frame, rows, cols, frame_size, rep_size, shard_width)
    back = jnp.swapaxes(back, 4, 5).reshape(1, per_frame, rows, cols, channels)
    return activations.astype(jnp.float32) + back.astype(jnp.float32) + temporal_bias


def shards(
    activations,
    spatial_weight,
    temporal_weight,
    first_gain,
    first_shift,
    spatial_bias,
    second_gain,
    second_shift,
    temporal_bias,
):
    rep_size = lax.axis_size("rep")
    frame_size = lax.axis_size("frame")
    row_size = lax.axis_size("row")
    frame_index = lax.axis_index("frame")
    row_index = lax.axis_index("row")
    channels = activations.shape[-1]
    rows = activations.shape[2]
    cols = activations.shape[3]
    width = channels // GROUPS
    shard_width = spatial_weight.shape[-1]

    spatial_w = gather_rep(spatial_weight)
    temporal_w = gather_rep(temporal_weight)
    local = spatial_w.shape[-1]

    raw = lax.all_gather(activations, "frame", axis=1, tiled=True)
    frames = raw.shape[1]

    if row_size > 1:
        down = [(i, i + 1) for i in range(row_size - 1)]
        up = [(i + 1, i) for i in range(row_size - 1)]
        above = lax.ppermute(raw[:, :, rows - 1 :], "row", down)
        below = lax.ppermute(raw[:, :, :1], "row", up)
    else:
        above = jnp.zeros_like(raw[:, :, :1])
        below = jnp.zeros_like(raw[:, :, :1])

    grouped = activations.astype(jnp.float32).reshape(1, -1, GROUPS, width)
    sums = jnp.sum(grouped, axis=(1, 3))
    squares = jnp.sum(grouped * grouped, axis=(1, 3))
    sums, squares = butterfly_sum((sums, squares), "frame")
    sums, squares = butterfly_sum((sums, squares), "row")
    count = grouped.shape[1] * width * frame_size * row_size
    mean = sums / count
    variance = squares / count - mean * mean
    inverse = lax.rsqrt(variance + EPS)
    mean_full = jnp.repeat(mean, width, axis=1)[:, None, None, None, :]
    inverse_full = jnp.repeat(inverse, width, axis=1)[:, None, None, None, :]

    def first_norm(x):
        normed = (x.astype(jnp.float32) - mean_full) * inverse_full * first_gain + first_shift
        return silu_bf16(normed)

    first_mid = first_norm(raw)
    first_above = jnp.where(row_index > 0, first_norm(above), jnp.zeros((), jnp.bfloat16))
    first_below = jnp.where(
        row_index < row_size - 1, first_norm(below), jnp.zeros((), jnp.bfloat16)
    )
    padded = jnp.concatenate([first_above, first_mid, first_below], axis=2)

    field = lax.optimization_barrier(padded[0])
    wide = spatial_w.reshape(3, 3, channels, local).transpose(0, 2, 1, 3)
    wide = wide.reshape(3, channels, 3 * local)
    product = None
    for row_tap in range(3):
        term = jnp.einsum(
            "frxc,cn->frxn",
            field[:, row_tap : row_tap + rows],
            wide[row_tap],
            preferred_element_type=jnp.float32,
        )
        product = term if product is None else product + term
    left = jnp.pad(product[:, :, :-1, :local], ((0, 0), (0, 0), (1, 0), (0, 0)))
    right = jnp.pad(product[:, :, 1:, 2 * local :], ((0, 0), (0, 0), (0, 1), (0, 0)))
    spatial = (left + product[..., local : 2 * local] + right)[None]
    spatial = spatial + local_vector(spatial_bias, frame_index, rep_size, frame_size)

    g2 = local_vector(second_gain, frame_index, rep_size, frame_size)
    s2 = local_vector(second_shift, frame_index, rep_size, frame_size)
    if shard_width % width == 0:
        grouped2 = spatial.reshape(-1, local // width, width)
        sums2 = jnp.sum(grouped2, axis=(0, 2))
        squares2 = jnp.sum(grouped2 * grouped2, axis=(0, 2))
        sums2, squares2 = pair_sum((sums2, squares2), "row")
        count2 = grouped2.shape[0] * width * row_size
        mean2 = sums2 / count2
        variance2 = squares2 / count2 - mean2 * mean2
        inverse2 = lax.rsqrt(variance2 + EPS)
        mean2_full = jnp.repeat(mean2, width)
        inverse2_full = jnp.repeat(inverse2, width)
    else:
        flat = spatial.reshape(-1, local)
        csum = jnp.sum(flat, axis=0)
        csq = jnp.sum(flat * flat, axis=0)
        csum, csq = pair_sum((csum, csq), "row")
        both = lax.all_gather(jnp.stack([csum, csq]), "frame", axis=0)
        both = both.reshape(frame_size, 2, rep_size, shard_width)
        both = jnp.transpose(both, (1, 2, 0, 3)).reshape(2, GROUPS, -1)
        gsum = jnp.sum(both, axis=2)
        count2 = flat.shape[0] * row_size * width
        gmean = gsum[0] / count2
        gvar = gsum[1] / count2 - gmean * gmean
        ginv = lax.rsqrt(gvar + EPS)
        mean2_full = local_vector(jnp.repeat(gmean, width), frame_index, rep_size, frame_size)
        inverse2_full = local_vector(jnp.repeat(ginv, width), frame_index, rep_size, frame_size)
    second = silu_bf16((spatial - mean2_full) * inverse2_full * g2 + s2)

    if frame_size > 8:
        return temporal_wide(activations, second, temporal_w, temporal_bias)
    second_all = lax.all_gather(second[0], "frame", axis=0, tiled=False)
    taps = temporal_w.reshape(3, rep_size, frame_size, shard_width, local)
    total = None
    for group in range(frame_size):
        weights = taps[:, :, group].reshape(3, rep_size * shard_width, local)
        weights = weights.transpose(1, 0, 2).reshape(rep_size * shard_width, 3 * local)
        term = jnp.einsum(
            "frxc,cn->frxn", second_all[group], weights, preferred_element_type=jnp.float32
        )
        total = term if total is None else total + term
    temporal = total[..., local : 2 * local]
    if frames > 1:
        before = jnp.pad(total[:-1, ..., :local], ((1, 0), (0, 0), (0, 0), (0, 0)))
        after = jnp.pad(total[1:, ..., 2 * local :], ((0, 1), (0, 0), (0, 0), (0, 0)))
        temporal = before + temporal + after
    temporal = temporal.astype(jnp.bfloat16)

    per_frame = frames // frame_size
    pieces = []
    for shift in range(frame_size):
        target = (frame_index + shift) % frame_size
        piece = lax.dynamic_slice_in_dim(temporal, target * per_frame, per_frame, axis=0)
        if shift:
            piece = lax.ppermute(
                piece, "frame", [(k, (k + shift) % frame_size) for k in range(frame_size)]
            )
        pieces.append(piece.reshape(per_frame, rows, cols, rep_size, shard_width))
    slots = []
    for group in range(frame_size):
        wanted = (frame_index - group) % frame_size
        slot = pieces[frame_size - 1]
        for shift in range(frame_size - 2, -1, -1):
            slot = jnp.where(wanted == shift, pieces[shift], slot)
        slots.append(slot)
    result = jnp.stack(slots, axis=4).reshape(1, per_frame, rows, cols, channels)
    return activations.astype(jnp.float32) + result.astype(jnp.float32) + temporal_bias


def solution(mesh):
    placed = (
        P("rep", "frame", "row", None, None),
        P(None, None, ("rep", "frame")),
        P(None, None, ("rep", "frame")),
        P(),
        P(),
        P(),
        P(),
        P(),
        P(),
    )

    return jax.shard_map(
        shards,
        mesh=mesh,
        in_specs=placed,
        out_specs=P("rep", "frame", "row", None, None),
        check_vma=False,
    )
```

```python
import numpy as np

import jax
import jax.numpy as jnp
from jax import lax
from jax.sharding import PartitionSpec as P


GROUPS = 32


EPS = 1e-05


def pair_sum(value, axis):
    if lax.axis_size(axis) == 2:
        return jax.tree.map(
            lambda v: v + lax.ppermute(v, axis, [(0, 1), (1, 0)]), value
        )
    return lax.psum(value, axis)


def butterfly_sum(value, axis):
    size = lax.axis_size(axis)
    if size & (size - 1) != 0:
        return lax.psum(value, axis)
    step = 1
    while step < size:
        pairs = [(k, k ^ step) for k in range(size)]
        value = jax.tree.map(lambda v: v + lax.ppermute(v, axis, pairs), value)
        step *= 2
    return value


def gather_rep(w):
    size = lax.axis_size("rep")
    if size != 4:
        return lax.all_gather(w, "rep", axis=w.ndim - 1, tiled=True)
    index = lax.axis_index("rep")
    across = lax.ppermute(w, "rep", [(k, k ^ 2) for k in range(size)])
    partner = lax.ppermute(w, "rep", [(k, k ^ 1) for k in range(size)])
    diagonal = lax.ppermute(across, "rep", [(k, k ^ 1) for k in range(size)])
    held = [w, partner, across, diagonal]
    blocks = []
    for position in range(size):
        offset = index ^ position
        block = held[3]
        for d in (2, 1, 0):
            block = jnp.where(offset == d, held[d], block)
        blocks.append(block)
    return jnp.concatenate(blocks, axis=-1)


def local_vector(vec, frame_index, rep_size, frame_size):
    width = vec.shape[0] // (rep_size * frame_size)
    table = vec.reshape(rep_size, frame_size, width)
    return lax.dynamic_index_in_dim(table, frame_index, axis=1, keepdims=False).reshape(-1)


def silu_bf16(normed):
    return jax.nn.silu(normed).astype(jnp.bfloat16)


def temporal_wide(activations, second, temporal_w, temporal_bias):
    rep_size = lax.axis_size("rep")
    frame_size = lax.axis_size("frame")
    channels = activations.shape[-1]
    _, frames, rows, cols, local = second.shape
    shard_width = local // rep_size
    second_all = lax.all_gather(second, "frame", axis=4, tiled=True)
    rows_order = np.arange(channels).reshape(rep_size, frame_size, shard_width)
    rows_order = rows_order.transpose(1, 0, 2).reshape(-1)
    temporal_w = temporal_w[:, rows_order, :]
    lhs_t = second_all.reshape(frames, rows * cols, channels)[None]
    kernel_t = temporal_w.reshape(3, 1, channels, local)
    temporal = lax.conv_general_dilated(
        lhs_t,
        kernel_t,
        window_strides=(1, 1),
        padding=((1, 1), (0, 0)),
        dimension_numbers=("NHWC", "HWIO", "NHWC"),
        preferred_element_type=jnp.float32,
    )
    temporal = temporal.reshape(1, frames, rows, cols, local).astype(jnp.bfloat16)
    back = lax.all_to_all(temporal, "frame", split_axis=1, concat_axis=4, tiled=True)
    per_frame = frames // frame_size
    back = back.reshape(1, per_frame, rows, cols, frame_size, rep_size, shard_width)
    back = jnp.swapaxes(back, 4, 5).reshape(1, per_frame, rows, cols, channels)
    return activations.astype(jnp.float32) + back.astype(jnp.float32) + temporal_bias


def shards(
    activations,
    spatial_weight,
    temporal_weight,
    first_gain,
    first_shift,
    spatial_bias,
    second_gain,
    second_shift,
    temporal_bias,
):
    rep_size = lax.axis_size("rep")
    frame_size = lax.axis_size("frame")
    row_size = lax.axis_size("row")
    frame_index = lax.axis_index("frame")
    row_index = lax.axis_index("row")
    channels = activations.shape[-1]
    rows = activations.shape[2]
    cols = activations.shape[3]
    width = channels // GROUPS
    shard_width = spatial_weight.shape[-1]

    spatial_shard = spatial_weight.reshape(3, 3, channels, shard_width).transpose(0, 2, 1, 3)
    spatial_w = gather_rep(spatial_shard)
    temporal_w = gather_rep(temporal_weight)
    local = rep_size * shard_width

    raw = lax.all_gather(activations, "frame", axis=1, tiled=True)
    frames = raw.shape[1]

    if row_size > 1:
        down = [(i, i + 1) for i in range(row_size - 1)]
        up = [(i + 1, i) for i in range(row_size - 1)]
        above = lax.ppermute(raw[:, :, rows - 1 :], "row", down)
        below = lax.ppermute(raw[:, :, :1], "row", up)
    else:
        above = jnp.zeros_like(raw[:, :, :1])
        below = jnp.zeros_like(raw[:, :, :1])

    grouped = activations.astype(jnp.float32).reshape(1, -1, GROUPS, width)
    stats = jnp.concatenate(
        [jnp.sum(grouped, axis=(1, 3)), jnp.sum(grouped * grouped, axis=(1, 3))]
    )
    stats = butterfly_sum(butterfly_sum(stats, "frame"), "row")
    sums, squares = stats[:1], stats[1:]
    count = grouped.shape[1] * width * frame_size * row_size
    mean = sums / count
    variance = squares / count - mean * mean
    inverse = lax.rsqrt(variance + EPS)
    mean_full = jnp.repeat(mean, width, axis=1)[:, None, None, None, :]
    inverse_full = jnp.repeat(inverse, width, axis=1)[:, None, None, None, :]

    def first_norm(x):
        normed = (x.astype(jnp.float32) - mean_full) * inverse_full * first_gain + first_shift
        return silu_bf16(normed)

    first_mid = first_norm(raw)
    first_above = jnp.where(row_index > 0, first_norm(above), jnp.zeros((), jnp.bfloat16))
    first_below = jnp.where(
        row_index < row_size - 1, first_norm(below), jnp.zeros((), jnp.bfloat16)
    )
    padded = jnp.concatenate([first_above, first_mid, first_below], axis=2)

    field = lax.optimization_barrier(padded[0])
    wide = spatial_w.reshape(3, channels, 3 * local)
    product = None
    for row_tap in range(3):
        term = jnp.einsum(
            "frxc,cn->frxn",
            field[:, row_tap : row_tap + rows],
            wide[row_tap],
            preferred_element_type=jnp.float32,
        )
        product = term if product is None else product + term
    left = jnp.pad(product[:, :, :-1, :local], ((0, 0), (0, 0), (1, 0), (0, 0)))
    right = jnp.pad(product[:, :, 1:, 2 * local :], ((0, 0), (0, 0), (0, 1), (0, 0)))
    spatial = (left + product[..., local : 2 * local] + right)[None]
    spatial = spatial + local_vector(spatial_bias, frame_index, rep_size, frame_size)

    g2 = local_vector(second_gain, frame_index, rep_size, frame_size)
    s2 = local_vector(second_shift, frame_index, rep_size, frame_size)
    if shard_width % width == 0:
        grouped2 = spatial.reshape(-1, local // width, width)
        stats2 = jnp.stack(
            [jnp.sum(grouped2, axis=(0, 2)), jnp.sum(grouped2 * grouped2, axis=(0, 2))]
        )
        stats2 = pair_sum(stats2, "row")
        sums2, squares2 = stats2[0], stats2[1]
        count2 = grouped2.shape[0] * width * row_size
        mean2 = sums2 / count2
        variance2 = squares2 / count2 - mean2 * mean2
        inverse2 = lax.rsqrt(variance2 + EPS)
        mean2_full = jnp.repeat(mean2, width)
        inverse2_full = jnp.repeat(inverse2, width)
    else:
        flat = spatial.reshape(-1, local)
        csum = jnp.sum(flat, axis=0)
        csq = jnp.sum(flat * flat, axis=0)
        csum, csq = pair_sum((csum, csq), "row")
        both = lax.all_gather(jnp.stack([csum, csq]), "frame", axis=0)
        both = both.reshape(frame_size, 2, rep_size, shard_width)
        both = jnp.transpose(both, (1, 2, 0, 3)).reshape(2, GROUPS, -1)
        gsum = jnp.sum(both, axis=2)
        count2 = flat.shape[0] * row_size * width
        gmean = gsum[0] / count2
        gvar = gsum[1] / count2 - gmean * gmean
        ginv = lax.rsqrt(gvar + EPS)
        mean2_full = local_vector(jnp.repeat(gmean, width), frame_index, rep_size, frame_size)
        inverse2_full = local_vector(jnp.repeat(ginv, width), frame_index, rep_size, frame_size)
    second = silu_bf16((spatial - mean2_full) * inverse2_full * g2 + s2)

    if frame_size > 8:
        return temporal_wide(activations, second, temporal_w, temporal_bias)
    second_all = lax.all_gather(second[0], "frame", axis=0, tiled=False)
    taps = temporal_w.reshape(3, rep_size, frame_size, shard_width, local)
    total = None
    for group in range(frame_size):
        weights = taps[:, :, group].reshape(3, rep_size * shard_width, local)
        weights = weights.transpose(1, 0, 2).reshape(rep_size * shard_width, 3 * local)
        term = jnp.einsum(
            "frxc,cn->frxn", second_all[group], weights, preferred_element_type=jnp.float32
        )
        total = term if total is None else total + term
    temporal = total[..., local : 2 * local]
    if frames > 1:
        before = jnp.pad(total[:-1, ..., :local], ((1, 0), (0, 0), (0, 0), (0, 0)))
        after = jnp.pad(total[1:, ..., 2 * local :], ((0, 1), (0, 0), (0, 0), (0, 0)))
        temporal = before + temporal + after
    temporal = temporal.astype(jnp.bfloat16)

    per_frame = frames // frame_size
    pieces = []
    for shift in range(frame_size):
        target = (frame_index + shift) % frame_size
        piece = lax.dynamic_slice_in_dim(temporal, target * per_frame, per_frame, axis=0)
        if shift:
            piece = lax.ppermute(
                piece, "frame", [(k, (k + shift) % frame_size) for k in range(frame_size)]
            )
        pieces.append(piece.reshape(per_frame, rows, cols, rep_size, shard_width))
    slots = []
    for group in range(frame_size):
        wanted = (frame_index - group) % frame_size
        slot = pieces[frame_size - 1]
        for shift in range(frame_size - 2, -1, -1):
            slot = jnp.where(wanted == shift, pieces[shift], slot)
        slots.append(slot)
    result = jnp.stack(slots, axis=4).reshape(1, per_frame, rows, cols, channels)
    return activations.astype(jnp.float32) + result.astype(jnp.float32) + temporal_bias


def solution(mesh):
    placed = (
        P("rep", "frame", "row", None, None),
        P(None, None, ("rep", "frame")),
        P(None, None, ("rep", "frame")),
        P(),
        P(),
        P(),
        P(),
        P(),
        P(),
    )

    return jax.shard_map(
        shards,
        mesh=mesh,
        in_specs=placed,
        out_specs=P("rep", "frame", "row", None, None),
        check_vma=False,
    )
```

```python
import numpy as np

import jax
import jax.numpy as jnp
from jax import lax
from jax.sharding import PartitionSpec as P


GROUPS = 32


EPS = 1e-05


def pair_sum(value, axis):
    if lax.axis_size(axis) == 2:
        return jax.tree.map(
            lambda v: v + lax.ppermute(v, axis, [(0, 1), (1, 0)]), value
        )
    return lax.psum(value, axis)


def gather_rep(w):
    size = lax.axis_size("rep")
    if size != 4:
        return lax.all_gather(w, "rep", axis=w.ndim - 1, tiled=True)
    index = lax.axis_index("rep")
    across = lax.ppermute(w, "rep", [(k, k ^ 2) for k in range(size)])
    partner = lax.ppermute(w, "rep", [(k, k ^ 1) for k in range(size)])
    diagonal = lax.ppermute(across, "rep", [(k, k ^ 1) for k in range(size)])
    held = [w, partner, across, diagonal]
    blocks = []
    for position in range(size):
        offset = index ^ position
        block = held[3]
        for d in (2, 1, 0):
            block = jnp.where(offset == d, held[d], block)
        blocks.append(block)
    return jnp.concatenate(blocks, axis=-1)


def local_vector(vec, frame_index, rep_size, frame_size):
    width = vec.shape[0] // (rep_size * frame_size)
    table = vec.reshape(rep_size, frame_size, width)
    return lax.dynamic_index_in_dim(table, frame_index, axis=1, keepdims=False).reshape(-1)


def silu_bf16(normed):
    return jax.nn.silu(normed).astype(jnp.bfloat16)


def temporal_wide(activations, second, temporal_w, temporal_bias):
    rep_size = lax.axis_size("rep")
    frame_size = lax.axis_size("frame")
    channels = activations.shape[-1]
    _, frames, rows, cols, local = second.shape
    shard_width = local // rep_size
    second_all = lax.all_gather(second, "frame", axis=4, tiled=True)
    rows_order = np.arange(channels).reshape(rep_size, frame_size, shard_width)
    rows_order = rows_order.transpose(1, 0, 2).reshape(-1)
    temporal_w = temporal_w[:, rows_order, :]
    lhs_t = second_all.reshape(frames, rows * cols, channels)[None]
    kernel_t = temporal_w.reshape(3, 1, channels, local)
    temporal = lax.conv_general_dilated(
        lhs_t,
        kernel_t,
        window_strides=(1, 1),
        padding=((1, 1), (0, 0)),
        dimension_numbers=("NHWC", "HWIO", "NHWC"),
        preferred_element_type=jnp.float32,
    )
    temporal = temporal.reshape(1, frames, rows, cols, local).astype(jnp.bfloat16)
    back = lax.all_to_all(temporal, "frame", split_axis=1, concat_axis=4, tiled=True)
    per_frame = frames // frame_size
    back = back.reshape(1, per_frame, rows, cols, frame_size, rep_size, shard_width)
    back = jnp.swapaxes(back, 4, 5).reshape(1, per_frame, rows, cols, channels)
    return activations.astype(jnp.float32) + back.astype(jnp.float32) + temporal_bias


def shards(
    activations,
    spatial_weight,
    temporal_weight,
    first_gain,
    first_shift,
    spatial_bias,
    second_gain,
    second_shift,
    temporal_bias,
):
    rep_size = lax.axis_size("rep")
    frame_size = lax.axis_size("frame")
    row_size = lax.axis_size("row")
    frame_index = lax.axis_index("frame")
    row_index = lax.axis_index("row")
    channels = activations.shape[-1]
    rows = activations.shape[2]
    cols = activations.shape[3]
    width = channels // GROUPS
    shard_width = spatial_weight.shape[-1]

    spatial_shard = spatial_weight.reshape(3, 3, channels, shard_width).transpose(0, 2, 1, 3)
    spatial_w = gather_rep(spatial_shard)
    temporal_w = gather_rep(temporal_weight)
    local = rep_size * shard_width

    raw = lax.all_gather(activations, "frame", axis=1, tiled=True)
    frames = raw.shape[1]

    if row_size > 1:
        down = [(i, i + 1) for i in range(row_size - 1)]
        up = [(i + 1, i) for i in range(row_size - 1)]
        above = lax.ppermute(raw[:, :, rows - 1 :], "row", down)
        below = lax.ppermute(raw[:, :, :1], "row", up)
    else:
        above = jnp.zeros_like(raw[:, :, :1])
        below = jnp.zeros_like(raw[:, :, :1])

    grouped = raw.astype(jnp.float32).reshape(1, -1, GROUPS, width)
    stats = jnp.concatenate(
        [jnp.sum(grouped, axis=(1, 3)), jnp.sum(grouped * grouped, axis=(1, 3))]
    )
    stats = pair_sum(stats, "row")
    sums, squares = stats[:1], stats[1:]
    count = grouped.shape[1] * width * row_size
    mean = sums / count
    variance = squares / count - mean * mean
    inverse = lax.rsqrt(variance + EPS)
    mean_full = jnp.repeat(mean, width, axis=1)[:, None, None, None, :]
    inverse_full = jnp.repeat(inverse, width, axis=1)[:, None, None, None, :]

    def first_norm(x):
        normed = (x.astype(jnp.float32) - mean_full) * inverse_full * first_gain + first_shift
        return silu_bf16(normed)

    first_mid = first_norm(raw)
    first_above = jnp.where(row_index > 0, first_norm(above), jnp.zeros((), jnp.bfloat16))
    first_below = jnp.where(
        row_index < row_size - 1, first_norm(below), jnp.zeros((), jnp.bfloat16)
    )
    padded = jnp.concatenate([first_above, first_mid, first_below], axis=2)

    field = lax.optimization_barrier(padded[0])
    wide = spatial_w.reshape(3, channels, 3 * local)
    product = None
    for row_tap in range(3):
        term = jnp.einsum(
            "frxc,cn->frxn",
            field[:, row_tap : row_tap + rows],
            wide[row_tap],
            preferred_element_type=jnp.float32,
        )
        product = term if product is None else product + term
    left = jnp.pad(product[:, :, :-1, :local], ((0, 0), (0, 0), (1, 0), (0, 0)))
    right = jnp.pad(product[:, :, 1:, 2 * local :], ((0, 0), (0, 0), (0, 1), (0, 0)))
    spatial = (left + product[..., local : 2 * local] + right)[None]
    spatial = spatial + local_vector(spatial_bias, frame_index, rep_size, frame_size)

    g2 = local_vector(second_gain, frame_index, rep_size, frame_size)
    s2 = local_vector(second_shift, frame_index, rep_size, frame_size)
    if shard_width % width == 0:
        grouped2 = spatial.reshape(-1, local // width, width)
        stats2 = jnp.stack(
            [jnp.sum(grouped2, axis=(0, 2)), jnp.sum(grouped2 * grouped2, axis=(0, 2))]
        )
        stats2 = pair_sum(stats2, "row")
        sums2, squares2 = stats2[0], stats2[1]
        count2 = grouped2.shape[0] * width * row_size
        mean2 = sums2 / count2
        variance2 = squares2 / count2 - mean2 * mean2
        inverse2 = lax.rsqrt(variance2 + EPS)
        mean2_full = jnp.repeat(mean2, width)
        inverse2_full = jnp.repeat(inverse2, width)
    else:
        flat = spatial.reshape(-1, local)
        csum = jnp.sum(flat, axis=0)
        csq = jnp.sum(flat * flat, axis=0)
        csum, csq = pair_sum((csum, csq), "row")
        both = lax.all_gather(jnp.stack([csum, csq]), "frame", axis=0)
        both = both.reshape(frame_size, 2, rep_size, shard_width)
        both = jnp.transpose(both, (1, 2, 0, 3)).reshape(2, GROUPS, -1)
        gsum = jnp.sum(both, axis=2)
        count2 = flat.shape[0] * row_size * width
        gmean = gsum[0] / count2
        gvar = gsum[1] / count2 - gmean * gmean
        ginv = lax.rsqrt(gvar + EPS)
        mean2_full = local_vector(jnp.repeat(gmean, width), frame_index, rep_size, frame_size)
        inverse2_full = local_vector(jnp.repeat(ginv, width), frame_index, rep_size, frame_size)
    second = silu_bf16((spatial - mean2_full) * inverse2_full * g2 + s2)

    if frame_size > 8:
        return temporal_wide(activations, second, temporal_w, temporal_bias)
    second_all = lax.all_gather(second[0], "frame", axis=0, tiled=False)
    taps = temporal_w.reshape(3, rep_size, frame_size, shard_width, local)
    total = None
    for group in range(frame_size):
        weights = taps[:, :, group].reshape(3, rep_size * shard_width, local)
        weights = weights.transpose(1, 0, 2).reshape(rep_size * shard_width, 3 * local)
        term = jnp.einsum(
            "frxc,cn->frxn", second_all[group], weights, preferred_element_type=jnp.float32
        )
        total = term if total is None else total + term
    temporal = total[..., local : 2 * local]
    if frames > 1:
        before = jnp.pad(total[:-1, ..., :local], ((1, 0), (0, 0), (0, 0), (0, 0)))
        after = jnp.pad(total[1:, ..., 2 * local :], ((0, 1), (0, 0), (0, 0), (0, 0)))
        temporal = before + temporal + after
    temporal = temporal.astype(jnp.bfloat16)

    per_frame = frames // frame_size
    pieces = []
    for shift in range(frame_size):
        target = (frame_index + shift) % frame_size
        piece = lax.dynamic_slice_in_dim(temporal, target * per_frame, per_frame, axis=0)
        if shift:
            piece = lax.ppermute(
                piece, "frame", [(k, (k + shift) % frame_size) for k in range(frame_size)]
            )
        pieces.append(piece.reshape(per_frame, rows, cols, rep_size, shard_width))
    slots = []
    for group in range(frame_size):
        wanted = (frame_index - group) % frame_size
        slot = pieces[frame_size - 1]
        for shift in range(frame_size - 2, -1, -1):
            slot = jnp.where(wanted == shift, pieces[shift], slot)
        slots.append(slot)
    result = jnp.stack(slots, axis=4).reshape(1, per_frame, rows, cols, channels)
    return activations.astype(jnp.float32) + result.astype(jnp.float32) + temporal_bias


def solution(mesh):
    placed = (
        P("rep", "frame", "row", None, None),
        P(None, None, ("rep", "frame")),
        P(None, None, ("rep", "frame")),
        P(),
        P(),
        P(),
        P(),
        P(),
        P(),
    )

    return jax.shard_map(
        shards,
        mesh=mesh,
        in_specs=placed,
        out_specs=P("rep", "frame", "row", None, None),
        check_vma=False,
    )
```

```python
import numpy as np

import jax
import jax.numpy as jnp
from jax import lax
from jax.sharding import PartitionSpec as P


GROUPS = 32


EPS = 1e-05


def pair_sum(value, axis):
    if lax.axis_size(axis) == 2:
        return jax.tree.map(
            lambda v: v + lax.ppermute(v, axis, [(0, 1), (1, 0)]), value
        )
    return lax.psum(value, axis)


def gather_rep(w):
    size = lax.axis_size("rep")
    if size != 4:
        return lax.all_gather(w, "rep", axis=w.ndim - 1, tiled=True)
    index = lax.axis_index("rep")
    across = lax.ppermute(w, "rep", [(k, k ^ 2) for k in range(size)])
    partner = lax.ppermute(w, "rep", [(k, k ^ 1) for k in range(size)])
    diagonal = lax.ppermute(across, "rep", [(k, k ^ 1) for k in range(size)])
    held = [w, partner, across, diagonal]
    blocks = []
    for position in range(size):
        offset = index ^ position
        block = held[3]
        for d in (2, 1, 0):
            block = jnp.where(offset == d, held[d], block)
        blocks.append(block)
    return jnp.concatenate(blocks, axis=-1)


def local_vector(vec, frame_index, rep_size, frame_size):
    width = vec.shape[0] // (rep_size * frame_size)
    table = vec.reshape(rep_size, frame_size, width)
    return lax.dynamic_index_in_dim(table, frame_index, axis=1, keepdims=False).reshape(-1)


def silu_bf16(normed):
    return jax.nn.silu(normed).astype(jnp.bfloat16)


def temporal_wide(activations, second, temporal_w, temporal_bias):
    rep_size = lax.axis_size("rep")
    frame_size = lax.axis_size("frame")
    channels = activations.shape[-1]
    _, frames, rows, cols, local = second.shape
    shard_width = local // rep_size
    second_all = lax.all_gather(second, "frame", axis=4, tiled=True)
    rows_order = np.arange(channels).reshape(rep_size, frame_size, shard_width)
    rows_order = rows_order.transpose(1, 0, 2).reshape(-1)
    temporal_w = temporal_w[:, rows_order, :]
    lhs_t = second_all.reshape(frames, rows * cols, channels)[None]
    kernel_t = temporal_w.reshape(3, 1, channels, local)
    temporal = lax.conv_general_dilated(
        lhs_t,
        kernel_t,
        window_strides=(1, 1),
        padding=((1, 1), (0, 0)),
        dimension_numbers=("NHWC", "HWIO", "NHWC"),
        preferred_element_type=jnp.float32,
    )
    temporal = temporal.reshape(1, frames, rows, cols, local).astype(jnp.bfloat16)
    back = lax.all_to_all(temporal, "frame", split_axis=1, concat_axis=4, tiled=True)
    per_frame = frames // frame_size
    back = back.reshape(1, per_frame, rows, cols, frame_size, rep_size, shard_width)
    back = jnp.swapaxes(back, 4, 5).reshape(1, per_frame, rows, cols, channels)
    return activations.astype(jnp.float32) + back.astype(jnp.float32) + temporal_bias


def shards(
    activations,
    spatial_weight,
    temporal_weight,
    first_gain,
    first_shift,
    spatial_bias,
    second_gain,
    second_shift,
    temporal_bias,
):
    rep_size = lax.axis_size("rep")
    frame_size = lax.axis_size("frame")
    row_size = lax.axis_size("row")
    frame_index = lax.axis_index("frame")
    row_index = lax.axis_index("row")
    channels = activations.shape[-1]
    rows = activations.shape[2]
    cols = activations.shape[3]
    width = channels // GROUPS
    shard_width = spatial_weight.shape[-1]

    spatial_shard = spatial_weight.reshape(3, 3, channels, shard_width).transpose(0, 2, 1, 3)
    spatial_w = gather_rep(spatial_shard)
    temporal_w = gather_rep(temporal_weight)
    local = rep_size * shard_width

    raw = lax.all_gather(activations, "frame", axis=1, tiled=True)
    frames = raw.shape[1]

    if row_size > 1:
        down = [(i, i + 1) for i in range(row_size - 1)]
        up = [(i + 1, i) for i in range(row_size - 1)]
        above = lax.ppermute(raw[:, :, rows - 1 :], "row", down)
        below = lax.ppermute(raw[:, :, :1], "row", up)
    else:
        above = jnp.zeros_like(raw[:, :, :1])
        below = jnp.zeros_like(raw[:, :, :1])

    grouped = raw.astype(jnp.float32).reshape(1, -1, GROUPS, width)
    stats = jnp.concatenate(
        [jnp.sum(grouped, axis=(1, 3)), jnp.sum(grouped * grouped, axis=(1, 3))]
    )
    stats = pair_sum(stats, "row")
    sums, squares = stats[:1], stats[1:]
    count = grouped.shape[1] * width * row_size
    mean = sums / count
    variance = squares / count - mean * mean
    inverse = lax.rsqrt(variance + EPS)
    mean_full = jnp.repeat(mean, width, axis=1)[:, None, None, None, :]
    inverse_full = jnp.repeat(inverse, width, axis=1)[:, None, None, None, :]

    def first_norm(x):
        normed = (x.astype(jnp.float32) - mean_full) * inverse_full * first_gain + first_shift
        return silu_bf16(normed)

    first_mid = first_norm(raw)
    first_above = jnp.where(row_index > 0, first_norm(above), jnp.zeros((), jnp.bfloat16))
    first_below = jnp.where(
        row_index < row_size - 1, first_norm(below), jnp.zeros((), jnp.bfloat16)
    )
    padded = jnp.concatenate([first_above, first_mid, first_below], axis=2)

    field = lax.optimization_barrier(padded[0])
    wide = spatial_w.reshape(3, channels, 3 * local)
    product = None
    for row_tap in range(3):
        term = jnp.einsum(
            "frxc,cn->frxn",
            field[:, row_tap : row_tap + rows],
            wide[row_tap],
            preferred_element_type=jnp.float32,
        )
        product = term if product is None else product + term
    left = jnp.pad(product[:, :, :-1, :local], ((0, 0), (0, 0), (1, 0), (0, 0)))
    right = jnp.pad(product[:, :, 1:, 2 * local :], ((0, 0), (0, 0), (0, 1), (0, 0)))
    spatial = (left + product[..., local : 2 * local] + right)[None]
    spatial = spatial + local_vector(spatial_bias, frame_index, rep_size, frame_size)

    g2 = local_vector(second_gain, frame_index, rep_size, frame_size)
    s2 = local_vector(second_shift, frame_index, rep_size, frame_size)
    if shard_width % width == 0:
        grouped2 = spatial.reshape(-1, local // width, width)
        stats2 = jnp.stack(
            [jnp.sum(grouped2, axis=(0, 2)), jnp.sum(grouped2 * grouped2, axis=(0, 2))]
        )
        stats2 = pair_sum(stats2, "row")
        sums2, squares2 = stats2[0], stats2[1]
        count2 = grouped2.shape[0] * width * row_size
        mean2 = sums2 / count2
        variance2 = squares2 / count2 - mean2 * mean2
        inverse2 = lax.rsqrt(variance2 + EPS)
        mean2_full = jnp.repeat(mean2, width)
        inverse2_full = jnp.repeat(inverse2, width)
    else:
        flat = spatial.reshape(-1, local)
        csum = jnp.sum(flat, axis=0)
        csq = jnp.sum(flat * flat, axis=0)
        csum, csq = pair_sum((csum, csq), "row")
        both = lax.all_gather(jnp.stack([csum, csq]), "frame", axis=0)
        both = both.reshape(frame_size, 2, rep_size, shard_width)
        both = jnp.transpose(both, (1, 2, 0, 3)).reshape(2, GROUPS, -1)
        gsum = jnp.sum(both, axis=2)
        count2 = flat.shape[0] * row_size * width
        gmean = gsum[0] / count2
        gvar = gsum[1] / count2 - gmean * gmean
        ginv = lax.rsqrt(gvar + EPS)
        mean2_full = local_vector(jnp.repeat(gmean, width), frame_index, rep_size, frame_size)
        inverse2_full = local_vector(jnp.repeat(ginv, width), frame_index, rep_size, frame_size)
    second = silu_bf16((spatial - mean2_full) * inverse2_full * g2 + s2)

    if frame_size > 8:
        return temporal_wide(activations, second, temporal_w, temporal_bias)
    taps = temporal_w.reshape(3, rep_size, frame_size, shard_width, local)
    wide_t = taps.transpose(2, 1, 3, 0, 4).reshape(frame_size, rep_size * shard_width, 3 * local)
    block = second[0]

    def product(source, group):
        weights = lax.dynamic_index_in_dim(wide_t, group, axis=0, keepdims=False)
        return jnp.einsum("frxc,cn->frxn", source, weights, preferred_element_type=jnp.float32)

    total = product(block, frame_index)
    for distance in range(1, frame_size):
        for sign in (1, -1):
            offset = sign * distance
            pairs = [
                (k + offset, k) for k in range(frame_size) if 0 <= k + offset < frame_size
            ]
            received = lax.ppermute(block, "frame", pairs)
            group = jnp.clip(frame_index + offset, 0, frame_size - 1)
            total = total + product(received, group)
    temporal = total[..., local : 2 * local]
    if frames > 1:
        before = jnp.pad(total[:-1, ..., :local], ((1, 0), (0, 0), (0, 0), (0, 0)))
        after = jnp.pad(total[1:, ..., 2 * local :], ((0, 1), (0, 0), (0, 0), (0, 0)))
        temporal = before + temporal + after
    temporal = temporal.astype(jnp.bfloat16)

    per_frame = frames // frame_size
    pieces = []
    for shift in range(frame_size):
        target = (frame_index + shift) % frame_size
        piece = lax.dynamic_slice_in_dim(temporal, target * per_frame, per_frame, axis=0)
        if shift:
            piece = lax.ppermute(
                piece, "frame", [(k, (k + shift) % frame_size) for k in range(frame_size)]
            )
        pieces.append(piece.reshape(per_frame, rows, cols, rep_size, shard_width))
    slots = []
    for group in range(frame_size):
        wanted = (frame_index - group) % frame_size
        slot = pieces[frame_size - 1]
        for shift in range(frame_size - 2, -1, -1):
            slot = jnp.where(wanted == shift, pieces[shift], slot)
        slots.append(slot)
    result = jnp.stack(slots, axis=4).reshape(1, per_frame, rows, cols, channels)
    return activations.astype(jnp.float32) + result.astype(jnp.float32) + temporal_bias


def solution(mesh):
    placed = (
        P("rep", "frame", "row", None, None),
        P(None, None, ("rep", "frame")),
        P(None, None, ("rep", "frame")),
        P(),
        P(),
        P(),
        P(),
        P(),
        P(),
    )

    return jax.shard_map(
        shards,
        mesh=mesh,
        in_specs=placed,
        out_specs=P("rep", "frame", "row", None, None),
        check_vma=False,
    )
```

```python
import numpy as np

import jax
import jax.numpy as jnp
from jax import lax
from jax.sharding import PartitionSpec as P


GROUPS = 32


EPS = 1e-05


def pair_sum(value, axis):
    if lax.axis_size(axis) == 2:
        return jax.tree.map(
            lambda v: v + lax.ppermute(v, axis, [(0, 1), (1, 0)]), value
        )
    return lax.psum(value, axis)


def gather_rep(w):
    size = lax.axis_size("rep")
    if size != 4:
        return lax.all_gather(w, "rep", axis=w.ndim - 1, tiled=True)
    index = lax.axis_index("rep")
    across = lax.ppermute(w, "rep", [(k, k ^ 2) for k in range(size)])
    partner = lax.ppermute(w, "rep", [(k, k ^ 1) for k in range(size)])
    diagonal = lax.ppermute(across, "rep", [(k, k ^ 1) for k in range(size)])
    held = [w, partner, across, diagonal]
    blocks = []
    for position in range(size):
        offset = index ^ position
        block = held[3]
        for d in (2, 1, 0):
            block = jnp.where(offset == d, held[d], block)
        blocks.append(block)
    return jnp.concatenate(blocks, axis=-1)


def local_vector(vec, frame_index, rep_size, frame_size):
    width = vec.shape[0] // (rep_size * frame_size)
    table = vec.reshape(rep_size, frame_size, width)
    return lax.dynamic_index_in_dim(table, frame_index, axis=1, keepdims=False).reshape(-1)


def silu_bf16(normed):
    return jax.nn.silu(normed).astype(jnp.bfloat16)


def temporal_wide(activations, second, temporal_w, temporal_bias):
    rep_size = lax.axis_size("rep")
    frame_size = lax.axis_size("frame")
    channels = activations.shape[-1]
    _, frames, rows, cols, local = second.shape
    shard_width = local // rep_size
    second_all = lax.all_gather(second, "frame", axis=4, tiled=True)
    rows_order = np.arange(channels).reshape(rep_size, frame_size, shard_width)
    rows_order = rows_order.transpose(1, 0, 2).reshape(-1)
    temporal_w = temporal_w[:, rows_order, :]
    lhs_t = second_all.reshape(frames, rows * cols, channels)[None]
    kernel_t = temporal_w.reshape(3, 1, channels, local)
    temporal = lax.conv_general_dilated(
        lhs_t,
        kernel_t,
        window_strides=(1, 1),
        padding=((1, 1), (0, 0)),
        dimension_numbers=("NHWC", "HWIO", "NHWC"),
        preferred_element_type=jnp.float32,
    )
    temporal = temporal.reshape(1, frames, rows, cols, local).astype(jnp.bfloat16)
    back = lax.all_to_all(temporal, "frame", split_axis=1, concat_axis=4, tiled=True)
    per_frame = frames // frame_size
    back = back.reshape(1, per_frame, rows, cols, frame_size, rep_size, shard_width)
    back = jnp.swapaxes(back, 4, 5).reshape(1, per_frame, rows, cols, channels)
    return activations.astype(jnp.float32) + back.astype(jnp.float32) + temporal_bias


def shards(
    activations,
    spatial_weight,
    temporal_weight,
    first_gain,
    first_shift,
    spatial_bias,
    second_gain,
    second_shift,
    temporal_bias,
):
    rep_size = lax.axis_size("rep")
    frame_size = lax.axis_size("frame")
    row_size = lax.axis_size("row")
    frame_index = lax.axis_index("frame")
    row_index = lax.axis_index("row")
    channels = activations.shape[-1]
    rows = activations.shape[2]
    cols = activations.shape[3]
    width = channels // GROUPS
    shard_width = spatial_weight.shape[-1]

    spatial_shard = spatial_weight.reshape(3, 3, channels, shard_width).transpose(0, 2, 1, 3)
    spatial_w = gather_rep(spatial_shard)
    temporal_w = gather_rep(temporal_weight)
    local = rep_size * shard_width

    raw = lax.all_gather(activations, "frame", axis=1, tiled=True)
    frames = raw.shape[1]

    if row_size > 1:
        down = [(i, i + 1) for i in range(row_size - 1)]
        up = [(i + 1, i) for i in range(row_size - 1)]
        above = lax.ppermute(raw[:, :, rows - 1 :], "row", down)
        below = lax.ppermute(raw[:, :, :1], "row", up)
    else:
        above = jnp.zeros_like(raw[:, :, :1])
        below = jnp.zeros_like(raw[:, :, :1])

    grouped = raw.astype(jnp.float32).reshape(1, -1, GROUPS, width)
    stats = jnp.concatenate(
        [jnp.sum(grouped, axis=(1, 3)), jnp.sum(grouped * grouped, axis=(1, 3))]
    )
    stats = pair_sum(stats, "row")
    sums, squares = stats[:1], stats[1:]
    count = grouped.shape[1] * width * row_size
    mean = sums / count
    variance = squares / count - mean * mean
    inverse = lax.rsqrt(variance + EPS)
    mean_full = jnp.repeat(mean, width, axis=1)[:, None, None, None, :]
    inverse_full = jnp.repeat(inverse, width, axis=1)[:, None, None, None, :]

    def first_norm(x):
        normed = (x.astype(jnp.float32) - mean_full) * inverse_full * first_gain + first_shift
        return silu_bf16(normed)

    first_mid = lax.optimization_barrier(first_norm(raw)[0])
    first_above = jnp.where(row_index > 0, first_norm(above), jnp.zeros((), jnp.bfloat16))[0]
    first_below = jnp.where(
        row_index < row_size - 1, first_norm(below), jnp.zeros((), jnp.bfloat16)
    )[0]

    wide = spatial_w.reshape(3, channels, 3 * local)

    def tap(field, row_tap):
        return jnp.einsum(
            "frxc,cn->frxn", field, wide[row_tap], preferred_element_type=jnp.float32
        )

    product = tap(first_mid, 1)
    product = product + jnp.pad(tap(first_mid[:, :-1], 0), ((0, 0), (1, 0), (0, 0), (0, 0)))
    product = product + jnp.pad(tap(first_mid[:, 1:], 2), ((0, 0), (0, 1), (0, 0), (0, 0)))
    product = product + jnp.pad(tap(first_above, 0), ((0, 0), (0, rows - 1), (0, 0), (0, 0)))
    product = product + jnp.pad(tap(first_below, 2), ((0, 0), (rows - 1, 0), (0, 0), (0, 0)))
    left = jnp.pad(product[:, :, :-1, :local], ((0, 0), (0, 0), (1, 0), (0, 0)))
    right = jnp.pad(product[:, :, 1:, 2 * local :], ((0, 0), (0, 0), (0, 1), (0, 0)))
    spatial = (left + product[..., local : 2 * local] + right)[None]
    spatial = spatial + local_vector(spatial_bias, frame_index, rep_size, frame_size)

    g2 = local_vector(second_gain, frame_index, rep_size, frame_size)
    s2 = local_vector(second_shift, frame_index, rep_size, frame_size)
    if shard_width % width == 0:
        grouped2 = spatial.reshape(-1, local // width, width)
        stats2 = jnp.stack(
            [jnp.sum(grouped2, axis=(0, 2)), jnp.sum(grouped2 * grouped2, axis=(0, 2))]
        )
        stats2 = pair_sum(stats2, "row")
        sums2, squares2 = stats2[0], stats2[1]
        count2 = grouped2.shape[0] * width * row_size
        mean2 = sums2 / count2
        variance2 = squares2 / count2 - mean2 * mean2
        inverse2 = lax.rsqrt(variance2 + EPS)
        mean2_full = jnp.repeat(mean2, width)
        inverse2_full = jnp.repeat(inverse2, width)
    else:
        flat = spatial.reshape(-1, local)
        csum = jnp.sum(flat, axis=0)
        csq = jnp.sum(flat * flat, axis=0)
        csum, csq = pair_sum((csum, csq), "row")
        both = lax.all_gather(jnp.stack([csum, csq]), "frame", axis=0)
        both = both.reshape(frame_size, 2, rep_size, shard_width)
        both = jnp.transpose(both, (1, 2, 0, 3)).reshape(2, GROUPS, -1)
        gsum = jnp.sum(both, axis=2)
        count2 = flat.shape[0] * row_size * width
        gmean = gsum[0] / count2
        gvar = gsum[1] / count2 - gmean * gmean
        ginv = lax.rsqrt(gvar + EPS)
        mean2_full = local_vector(jnp.repeat(gmean, width), frame_index, rep_size, frame_size)
        inverse2_full = local_vector(jnp.repeat(ginv, width), frame_index, rep_size, frame_size)
    second = silu_bf16((spatial - mean2_full) * inverse2_full * g2 + s2)

    if frame_size > 8:
        return temporal_wide(activations, second, temporal_w, temporal_bias)
    second_all = lax.all_gather(second[0], "frame", axis=0, tiled=False)
    taps = temporal_w.reshape(3, rep_size, frame_size, shard_width, local)
    total = None
    for group in range(frame_size):
        weights = taps[:, :, group].reshape(3, rep_size * shard_width, local)
        weights = weights.transpose(1, 0, 2).reshape(rep_size * shard_width, 3 * local)
        term = jnp.einsum(
            "frxc,cn->frxn", second_all[group], weights, preferred_element_type=jnp.float32
        )
        total = term if total is None else total + term
    temporal = total[..., local : 2 * local]
    if frames > 1:
        before = jnp.pad(total[:-1, ..., :local], ((1, 0), (0, 0), (0, 0), (0, 0)))
        after = jnp.pad(total[1:, ..., 2 * local :], ((0, 1), (0, 0), (0, 0), (0, 0)))
        temporal = before + temporal + after
    temporal = temporal.astype(jnp.bfloat16)

    per_frame = frames // frame_size
    pieces = []
    for shift in range(frame_size):
        target = (frame_index + shift) % frame_size
        piece = lax.dynamic_slice_in_dim(temporal, target * per_frame, per_frame, axis=0)
        if shift:
            piece = lax.ppermute(
                piece, "frame", [(k, (k + shift) % frame_size) for k in range(frame_size)]
            )
        pieces.append(piece.reshape(per_frame, rows, cols, rep_size, shard_width))
    slots = []
    for group in range(frame_size):
        wanted = (frame_index - group) % frame_size
        slot = pieces[frame_size - 1]
        for shift in range(frame_size - 2, -1, -1):
            slot = jnp.where(wanted == shift, pieces[shift], slot)
        slots.append(slot)
    result = jnp.stack(slots, axis=4).reshape(1, per_frame, rows, cols, channels)
    return activations.astype(jnp.float32) + result.astype(jnp.float32) + temporal_bias


def solution(mesh):
    placed = (
        P("rep", "frame", "row", None, None),
        P(None, None, ("rep", "frame")),
        P(None, None, ("rep", "frame")),
        P(),
        P(),
        P(),
        P(),
        P(),
        P(),
    )

    return jax.shard_map(
        shards,
        mesh=mesh,
        in_specs=placed,
        out_specs=P("rep", "frame", "row", None, None),
        check_vma=False,
    )
```

```python
import numpy as np

import jax
import jax.numpy as jnp
from jax import lax
from jax.sharding import PartitionSpec as P


GROUPS = 32


EPS = 1e-05


def pair_sum(value, axis):
    if lax.axis_size(axis) == 2:
        return jax.tree.map(
            lambda v: v + lax.ppermute(v, axis, [(0, 1), (1, 0)]), value
        )
    return lax.psum(value, axis)


def gather_rep(w):
    size = lax.axis_size("rep")
    if size != 4:
        return lax.all_gather(w, "rep", axis=w.ndim - 1, tiled=True)
    index = lax.axis_index("rep")
    across = lax.ppermute(w, "rep", [(k, k ^ 2) for k in range(size)])
    partner = lax.ppermute(w, "rep", [(k, k ^ 1) for k in range(size)])
    diagonal = lax.ppermute(across, "rep", [(k, k ^ 1) for k in range(size)])
    held = [w, partner, across, diagonal]
    blocks = []
    for position in range(size):
        offset = index ^ position
        block = held[3]
        for d in (2, 1, 0):
            block = jnp.where(offset == d, held[d], block)
        blocks.append(block)
    return jnp.concatenate(blocks, axis=-1)


def local_vector(vec, frame_index, rep_size, frame_size):
    width = vec.shape[0] // (rep_size * frame_size)
    table = vec.reshape(rep_size, frame_size, width)
    return lax.dynamic_index_in_dim(table, frame_index, axis=1, keepdims=False).reshape(-1)


def silu_bf16(normed):
    return jax.nn.silu(normed).astype(jnp.bfloat16)


def temporal_wide(activations, second, temporal_w, temporal_bias):
    rep_size = lax.axis_size("rep")
    frame_size = lax.axis_size("frame")
    channels = activations.shape[-1]
    _, frames, rows, cols, local = second.shape
    shard_width = local // rep_size
    second_all = lax.all_gather(second, "frame", axis=4, tiled=True)
    rows_order = np.arange(channels).reshape(rep_size, frame_size, shard_width)
    rows_order = rows_order.transpose(1, 0, 2).reshape(-1)
    temporal_w = temporal_w[:, rows_order, :]
    lhs_t = second_all.reshape(frames, rows * cols, channels)[None]
    kernel_t = temporal_w.reshape(3, 1, channels, local)
    temporal = lax.conv_general_dilated(
        lhs_t,
        kernel_t,
        window_strides=(1, 1),
        padding=((1, 1), (0, 0)),
        dimension_numbers=("NHWC", "HWIO", "NHWC"),
        preferred_element_type=jnp.float32,
    )
    temporal = temporal.reshape(1, frames, rows, cols, local).astype(jnp.bfloat16)
    back = lax.all_to_all(temporal, "frame", split_axis=1, concat_axis=4, tiled=True)
    per_frame = frames // frame_size
    back = back.reshape(1, per_frame, rows, cols, frame_size, rep_size, shard_width)
    back = jnp.swapaxes(back, 4, 5).reshape(1, per_frame, rows, cols, channels)
    return activations.astype(jnp.float32) + back.astype(jnp.float32) + temporal_bias


def shards(
    activations,
    spatial_weight,
    temporal_weight,
    first_gain,
    first_shift,
    spatial_bias,
    second_gain,
    second_shift,
    temporal_bias,
):
    rep_size = lax.axis_size("rep")
    frame_size = lax.axis_size("frame")
    row_size = lax.axis_size("row")
    frame_index = lax.axis_index("frame")
    row_index = lax.axis_index("row")
    channels = activations.shape[-1]
    rows = activations.shape[2]
    cols = activations.shape[3]
    width = channels // GROUPS
    shard_width = spatial_weight.shape[-1]

    spatial_shard = spatial_weight.reshape(3, 3, channels, shard_width).transpose(0, 2, 1, 3)
    spatial_w = gather_rep(spatial_shard)
    temporal_w = gather_rep(temporal_weight)
    local = rep_size * shard_width

    raw = lax.all_gather(activations, "frame", axis=1, tiled=True)
    frames = raw.shape[1]

    if row_size > 1:
        down = [(i, i + 1) for i in range(row_size - 1)]
        up = [(i + 1, i) for i in range(row_size - 1)]
        above = lax.ppermute(raw[:, :, rows - 1 :], "row", down)
        below = lax.ppermute(raw[:, :, :1], "row", up)
    else:
        above = jnp.zeros_like(raw[:, :, :1])
        below = jnp.zeros_like(raw[:, :, :1])

    grouped = raw.astype(jnp.float32).reshape(1, -1, GROUPS, width)
    stats = jnp.concatenate(
        [jnp.sum(grouped, axis=(1, 3)), jnp.sum(grouped * grouped, axis=(1, 3))]
    )
    stats = pair_sum(stats, "row")
    sums, squares = stats[:1], stats[1:]
    count = grouped.shape[1] * width * row_size
    mean = sums / count
    variance = squares / count - mean * mean
    inverse = lax.rsqrt(variance + EPS)
    mean_full = jnp.repeat(mean, width, axis=1)[:, None, None, None, :]
    inverse_full = jnp.repeat(inverse, width, axis=1)[:, None, None, None, :]

    def first_norm(x):
        normed = (x.astype(jnp.float32) - mean_full) * inverse_full * first_gain + first_shift
        return silu_bf16(normed)

    first_mid = lax.optimization_barrier(first_norm(raw)[0])
    first_above = jnp.where(row_index > 0, first_norm(above), jnp.zeros((), jnp.bfloat16))[0]
    first_below = jnp.where(
        row_index < row_size - 1, first_norm(below), jnp.zeros((), jnp.bfloat16)
    )[0]

    wide = spatial_w.reshape(3, channels, 3 * local)

    def tap(field, row_tap):
        return jnp.einsum(
            "frxc,cn->frxn", field, wide[row_tap], preferred_element_type=jnp.float32
        )

    product = tap(first_mid, 1)
    product = product + jnp.pad(tap(first_mid[:, :-1], 0), ((0, 0), (1, 0), (0, 0), (0, 0)))
    product = product + jnp.pad(tap(first_mid[:, 1:], 2), ((0, 0), (0, 1), (0, 0), (0, 0)))
    product = product + jnp.pad(tap(first_above, 0), ((0, 0), (0, rows - 1), (0, 0), (0, 0)))
    product = product + jnp.pad(tap(first_below, 2), ((0, 0), (rows - 1, 0), (0, 0), (0, 0)))
    left = jnp.pad(product[:, :, :-1, :local], ((0, 0), (0, 0), (1, 0), (0, 0)))
    right = jnp.pad(product[:, :, 1:, 2 * local :], ((0, 0), (0, 0), (0, 1), (0, 0)))
    spatial = (left + product[..., local : 2 * local] + right)[None]
    spatial = spatial + local_vector(spatial_bias, frame_index, rep_size, frame_size)

    g2 = local_vector(second_gain, frame_index, rep_size, frame_size)
    s2 = local_vector(second_shift, frame_index, rep_size, frame_size)
    if shard_width % width == 0:
        grouped2 = spatial.reshape(-1, local // width, width)
        stats2 = jnp.stack(
            [jnp.sum(grouped2, axis=(0, 2)), jnp.sum(grouped2 * grouped2, axis=(0, 2))]
        )
        stats2 = pair_sum(stats2, "row")
        sums2, squares2 = stats2[0], stats2[1]
        count2 = grouped2.shape[0] * width * row_size
        mean2 = sums2 / count2
        variance2 = squares2 / count2 - mean2 * mean2
        inverse2 = lax.rsqrt(variance2 + EPS)
        mean2_full = jnp.repeat(mean2, width)
        inverse2_full = jnp.repeat(inverse2, width)
    else:
        flat = spatial.reshape(-1, local)
        csum = jnp.sum(flat, axis=0)
        csq = jnp.sum(flat * flat, axis=0)
        csum, csq = pair_sum((csum, csq), "row")
        both = lax.all_gather(jnp.stack([csum, csq]), "frame", axis=0)
        both = both.reshape(frame_size, 2, rep_size, shard_width)
        both = jnp.transpose(both, (1, 2, 0, 3)).reshape(2, GROUPS, -1)
        gsum = jnp.sum(both, axis=2)
        count2 = flat.shape[0] * row_size * width
        gmean = gsum[0] / count2
        gvar = gsum[1] / count2 - gmean * gmean
        ginv = lax.rsqrt(gvar + EPS)
        mean2_full = local_vector(jnp.repeat(gmean, width), frame_index, rep_size, frame_size)
        inverse2_full = local_vector(jnp.repeat(ginv, width), frame_index, rep_size, frame_size)
    second = silu_bf16((spatial - mean2_full) * inverse2_full * g2 + s2)

    if frame_size > 8:
        return temporal_wide(activations, second, temporal_w, temporal_bias)
    second_all = lax.all_gather(second[0], "frame", axis=0, tiled=False)
    taps = temporal_w.reshape(3, rep_size, frame_size, shard_width, local)
    total = None
    for group in range(frame_size):
        weights = taps[:, :, group].reshape(3, rep_size * shard_width, local)
        weights = weights.transpose(1, 0, 2).reshape(rep_size * shard_width, 3 * local)
        term = jnp.einsum(
            "frxc,cn->frxn", second_all[group], weights, preferred_element_type=jnp.float32
        )
        total = term if total is None else total + term
    temporal = total[..., local : 2 * local]
    if frames > 1:
        before = jnp.pad(total[:-1, ..., :local], ((1, 0), (0, 0), (0, 0), (0, 0)))
        after = jnp.pad(total[1:, ..., 2 * local :], ((0, 1), (0, 0), (0, 0), (0, 0)))
        temporal = before + temporal + after
    temporal = temporal.astype(jnp.bfloat16)

    per_frame = frames // frame_size
    pieces = []
    for shift in range(frame_size):
        target = (frame_index + shift) % frame_size
        piece = lax.dynamic_slice_in_dim(temporal, target * per_frame, per_frame, axis=0)
        if shift:
            piece = lax.ppermute(
                piece, "frame", [(k, (k + shift) % frame_size) for k in range(frame_size)]
            )
        pieces.append(piece.reshape(per_frame, rows, cols, rep_size, shard_width))
    slots = []
    for group in range(frame_size):
        wanted = (frame_index - group) % frame_size
        slot = pieces[frame_size - 1]
        for shift in range(frame_size - 2, -1, -1):
            slot = jnp.where(wanted == shift, pieces[shift], slot)
        slots.append(slot)
    result = jnp.concatenate(
        [slots[group][..., block, :] for block in range(rep_size) for group in range(frame_size)],
        axis=-1,
    )[None]
    return activations.astype(jnp.float32) + result.astype(jnp.float32) + temporal_bias


def solution(mesh):
    placed = (
        P("rep", "frame", "row", None, None),
        P(None, None, ("rep", "frame")),
        P(None, None, ("rep", "frame")),
        P(),
        P(),
        P(),
        P(),
        P(),
        P(),
    )

    return jax.shard_map(
        shards,
        mesh=mesh,
        in_specs=placed,
        out_specs=P("rep", "frame", "row", None, None),
        check_vma=False,
    )
```

```python
import numpy as np

import jax
import jax.numpy as jnp
from jax import lax
from jax.sharding import PartitionSpec as P


GROUPS = 32


EPS = 1e-05


def pair_sum(value, axis):
    if lax.axis_size(axis) == 2:
        return jax.tree.map(
            lambda v: v + lax.ppermute(v, axis, [(0, 1), (1, 0)]), value
        )
    return lax.psum(value, axis)


def butterfly_sum(value, axis):
    size = lax.axis_size(axis)
    if size & (size - 1) != 0:
        return lax.psum(value, axis)
    step = 1
    while step < size:
        pairs = [(k, k ^ step) for k in range(size)]
        value = jax.tree.map(lambda v: v + lax.ppermute(v, axis, pairs), value)
        step *= 2
    return value


def gather_rep(w):
    size = lax.axis_size("rep")
    if size != 4:
        return lax.all_gather(w, "rep", axis=w.ndim - 1, tiled=True)
    index = lax.axis_index("rep")
    across = lax.ppermute(w, "rep", [(k, k ^ 2) for k in range(size)])
    partner = lax.ppermute(w, "rep", [(k, k ^ 1) for k in range(size)])
    diagonal = lax.ppermute(across, "rep", [(k, k ^ 1) for k in range(size)])
    held = [w, partner, across, diagonal]
    blocks = []
    for position in range(size):
        offset = index ^ position
        block = held[3]
        for d in (2, 1, 0):
            block = jnp.where(offset == d, held[d], block)
        blocks.append(block)
    return jnp.concatenate(blocks, axis=-1)


def local_vector(vec, frame_index, rep_size, frame_size):
    width = vec.shape[0] // (rep_size * frame_size)
    table = vec.reshape(rep_size, frame_size, width)
    return lax.dynamic_index_in_dim(table, frame_index, axis=1, keepdims=False).reshape(-1)


def silu_bf16(normed):
    return jax.nn.silu(normed).astype(jnp.bfloat16)


def temporal_wide(activations, second, temporal_w, temporal_bias):
    rep_size = lax.axis_size("rep")
    frame_size = lax.axis_size("frame")
    channels = activations.shape[-1]
    _, frames, rows, cols, local = second.shape
    shard_width = local // rep_size
    second_all = lax.all_gather(second, "frame", axis=4, tiled=True)
    rows_order = np.arange(channels).reshape(rep_size, frame_size, shard_width)
    rows_order = rows_order.transpose(1, 0, 2).reshape(-1)
    temporal_w = temporal_w[:, rows_order, :]
    lhs_t = second_all.reshape(frames, rows * cols, channels)[None]
    kernel_t = temporal_w.reshape(3, 1, channels, local)
    temporal = lax.conv_general_dilated(
        lhs_t,
        kernel_t,
        window_strides=(1, 1),
        padding=((1, 1), (0, 0)),
        dimension_numbers=("NHWC", "HWIO", "NHWC"),
        preferred_element_type=jnp.float32,
    )
    temporal = temporal.reshape(1, frames, rows, cols, local).astype(jnp.bfloat16)
    back = lax.all_to_all(temporal, "frame", split_axis=1, concat_axis=4, tiled=True)
    per_frame = frames // frame_size
    back = back.reshape(1, per_frame, rows, cols, frame_size, rep_size, shard_width)
    back = jnp.swapaxes(back, 4, 5).reshape(1, per_frame, rows, cols, channels)
    return activations.astype(jnp.float32) + back.astype(jnp.float32) + temporal_bias


def shards(
    activations,
    spatial_weight,
    temporal_weight,
    first_gain,
    first_shift,
    spatial_bias,
    second_gain,
    second_shift,
    temporal_bias,
):
    rep_size = lax.axis_size("rep")
    frame_size = lax.axis_size("frame")
    row_size = lax.axis_size("row")
    frame_index = lax.axis_index("frame")
    row_index = lax.axis_index("row")
    channels = activations.shape[-1]
    rows = activations.shape[2]
    cols = activations.shape[3]
    width = channels // GROUPS
    shard_width = spatial_weight.shape[-1]

    spatial_shard = spatial_weight.reshape(3, 3, channels, shard_width).transpose(0, 2, 1, 3)
    spatial_w = gather_rep(spatial_shard)
    temporal_w = gather_rep(temporal_weight)
    local = rep_size * shard_width

    raw = lax.all_gather(activations, "frame", axis=1, tiled=True)
    frames = raw.shape[1]

    if row_size > 1:
        down = [(i, i + 1) for i in range(row_size - 1)]
        up = [(i + 1, i) for i in range(row_size - 1)]
        above = lax.ppermute(raw[:, :, rows - 1 :], "row", down)
        below = lax.ppermute(raw[:, :, :1], "row", up)
    else:
        above = jnp.zeros_like(raw[:, :, :1])
        below = jnp.zeros_like(raw[:, :, :1])

    grouped = activations.astype(jnp.float32).reshape(1, -1, GROUPS, width)
    stats = jnp.concatenate(
        [jnp.sum(grouped, axis=(1, 3)), jnp.sum(grouped * grouped, axis=(1, 3))]
    )
    stats = butterfly_sum(butterfly_sum(stats, "frame"), "row")
    sums, squares = stats[:1] * 1.0, stats[1:]
    count = grouped.shape[1] * width * frame_size * row_size
    mean = sums / count
    variance = squares / count - mean * mean
    inverse = lax.rsqrt(variance + EPS)
    mean_full = jnp.repeat(mean, width, axis=1)[:, None, None, None, :]
    inverse_full = jnp.repeat(inverse, width, axis=1)[:, None, None, None, :]

    def first_norm(x):
        normed = (x.astype(jnp.float32) - mean_full) * inverse_full * first_gain + first_shift
        return silu_bf16(normed)

    first_mid = lax.optimization_barrier(first_norm(raw)[0])
    first_above = jnp.where(row_index > 0, first_norm(above), jnp.zeros((), jnp.bfloat16))[0]
    first_below = jnp.where(
        row_index < row_size - 1, first_norm(below), jnp.zeros((), jnp.bfloat16)
    )[0]

    wide = spatial_w.reshape(3, channels, 3 * local)

    def tap(field, row_tap):
        return jnp.einsum(
            "frxc,cn->frxn", field, wide[row_tap], preferred_element_type=jnp.float32
        )

    product = tap(first_mid, 1)
    product = product + jnp.pad(tap(first_mid[:, :-1], 0), ((0, 0), (1, 0), (0, 0), (0, 0)))
    product = product + jnp.pad(tap(first_mid[:, 1:], 2), ((0, 0), (0, 1), (0, 0), (0, 0)))
    product = product + jnp.pad(tap(first_above, 0), ((0, 0), (0, rows - 1), (0, 0), (0, 0)))
    product = product + jnp.pad(tap(first_below, 2), ((0, 0), (rows - 1, 0), (0, 0), (0, 0)))
    left = jnp.pad(product[:, :, :-1, :local], ((0, 0), (0, 0), (1, 0), (0, 0)))
    right = jnp.pad(product[:, :, 1:, 2 * local :], ((0, 0), (0, 0), (0, 1), (0, 0)))
    spatial = (left + product[..., local : 2 * local] + right)[None]
    spatial = spatial + local_vector(spatial_bias, frame_index, rep_size, frame_size)

    g2 = local_vector(second_gain, frame_index, rep_size, frame_size)
    s2 = local_vector(second_shift, frame_index, rep_size, frame_size)
    if shard_width % width == 0:
        grouped2 = spatial.reshape(-1, local // width, width)
        stats2 = jnp.stack(
            [jnp.sum(grouped2, axis=(0, 2)), jnp.sum(grouped2 * grouped2, axis=(0, 2))]
        )
        stats2 = pair_sum(stats2, "row")
        sums2, squares2 = stats2[0], stats2[1]
        count2 = grouped2.shape[0] * width * row_size
        mean2 = sums2 / count2
        variance2 = squares2 / count2 - mean2 * mean2
        inverse2 = lax.rsqrt(variance2 + EPS)
        mean2_full = jnp.repeat(mean2, width)
        inverse2_full = jnp.repeat(inverse2, width)
    else:
        flat = spatial.reshape(-1, local)
        csum = jnp.sum(flat, axis=0)
        csq = jnp.sum(flat * flat, axis=0)
        csum, csq = pair_sum((csum, csq), "row")
        both = lax.all_gather(jnp.stack([csum, csq]), "frame", axis=0)
        both = both.reshape(frame_size, 2, rep_size, shard_width)
        both = jnp.transpose(both, (1, 2, 0, 3)).reshape(2, GROUPS, -1)
        gsum = jnp.sum(both, axis=2)
        count2 = flat.shape[0] * row_size * width
        gmean = gsum[0] / count2
        gvar = gsum[1] / count2 - gmean * gmean
        ginv = lax.rsqrt(gvar + EPS)
        mean2_full = local_vector(jnp.repeat(gmean, width), frame_index, rep_size, frame_size)
        inverse2_full = local_vector(jnp.repeat(ginv, width), frame_index, rep_size, frame_size)
    second = silu_bf16((spatial - mean2_full) * inverse2_full * g2 + s2)

    if frame_size > 8:
        return temporal_wide(activations, second, temporal_w, temporal_bias)
    second_all = lax.all_gather(second[0], "frame", axis=0, tiled=False)
    taps = temporal_w.reshape(3, rep_size, frame_size, shard_width, local)
    total = None
    for group in range(frame_size):
        weights = taps[:, :, group].reshape(3, rep_size * shard_width, local)
        weights = weights.transpose(1, 0, 2).reshape(rep_size * shard_width, 3 * local)
        term = jnp.einsum(
            "frxc,cn->frxn", second_all[group], weights, preferred_element_type=jnp.float32
        )
        total = term if total is None else total + term
    temporal = total[..., local : 2 * local]
    if frames > 1:
        before = jnp.pad(total[:-1, ..., :local], ((1, 0), (0, 0), (0, 0), (0, 0)))
        after = jnp.pad(total[1:, ..., 2 * local :], ((0, 1), (0, 0), (0, 0), (0, 0)))
        temporal = before + temporal + after
    temporal = temporal.astype(jnp.bfloat16)

    per_frame = frames // frame_size
    pieces = []
    for shift in range(frame_size):
        target = (frame_index + shift) % frame_size
        piece = lax.dynamic_slice_in_dim(temporal, target * per_frame, per_frame, axis=0)
        if shift:
            piece = lax.ppermute(
                piece, "frame", [(k, (k + shift) % frame_size) for k in range(frame_size)]
            )
        pieces.append(piece.reshape(per_frame, rows, cols, rep_size, shard_width))
    slots = []
    for group in range(frame_size):
        wanted = (frame_index - group) % frame_size
        slot = pieces[frame_size - 1]
        for shift in range(frame_size - 2, -1, -1):
            slot = jnp.where(wanted == shift, pieces[shift], slot)
        slots.append(slot)
    result = jnp.concatenate(
        [slots[group][..., block, :] for block in range(rep_size) for group in range(frame_size)],
        axis=-1,
    )[None]
    return activations.astype(jnp.float32) + result.astype(jnp.float32) + temporal_bias


def solution(mesh):
    placed = (
        P("rep", "frame", "row", None, None),
        P(None, None, ("rep", "frame")),
        P(None, None, ("rep", "frame")),
        P(),
        P(),
        P(),
        P(),
        P(),
        P(),
    )

    return jax.shard_map(
        shards,
        mesh=mesh,
        in_specs=placed,
        out_specs=P("rep", "frame", "row", None, None),
        check_vma=False,
    )
```

```python
import numpy as np

import jax
import jax.numpy as jnp
from jax import lax
from jax.sharding import PartitionSpec as P


GROUPS = 32


EPS = 1e-05


def pair_sum(value, axis):
    if lax.axis_size(axis) == 2:
        return jax.tree.map(
            lambda v: v + lax.ppermute(v, axis, [(0, 1), (1, 0)]), value
        )
    return lax.psum(value, axis)


def butterfly_sum(value, axis):
    size = lax.axis_size(axis)
    if size & (size - 1) != 0:
        return lax.psum(value, axis)
    step = 1
    while step < size:
        pairs = [(k, k ^ step) for k in range(size)]
        value = jax.tree.map(lambda v: v + lax.ppermute(v, axis, pairs), value)
        step *= 2
    return value


def gather_rep(w):
    size = lax.axis_size("rep")
    if size != 4:
        return lax.all_gather(w, "rep", axis=w.ndim - 1, tiled=True)
    index = lax.axis_index("rep")
    across = lax.ppermute(w, "rep", [(k, k ^ 2) for k in range(size)])
    partner = lax.ppermute(w, "rep", [(k, k ^ 1) for k in range(size)])
    diagonal = lax.ppermute(across, "rep", [(k, k ^ 1) for k in range(size)])
    held = [w, partner, across, diagonal]
    blocks = []
    for position in range(size):
        offset = index ^ position
        block = held[3]
        for d in (2, 1, 0):
            block = jnp.where(offset == d, held[d], block)
        blocks.append(block)
    return jnp.concatenate(blocks, axis=-1)


def local_vector(vec, frame_index, rep_size, frame_size):
    width = vec.shape[0] // (rep_size * frame_size)
    table = vec.reshape(rep_size, frame_size, width)
    return lax.dynamic_index_in_dim(table, frame_index, axis=1, keepdims=False).reshape(-1)


def silu_bf16(normed):
    return jax.nn.silu(normed).astype(jnp.bfloat16)


def temporal_wide(activations, second, temporal_w, temporal_bias):
    rep_size = lax.axis_size("rep")
    frame_size = lax.axis_size("frame")
    channels = activations.shape[-1]
    _, frames, rows, cols, local = second.shape
    shard_width = local // rep_size
    second_all = lax.all_gather(second, "frame", axis=4, tiled=True)
    rows_order = np.arange(channels).reshape(rep_size, frame_size, shard_width)
    rows_order = rows_order.transpose(1, 0, 2).reshape(-1)
    temporal_w = temporal_w[:, rows_order, :]
    lhs_t = second_all.reshape(frames, rows * cols, channels)[None]
    kernel_t = temporal_w.reshape(3, 1, channels, local)
    temporal = lax.conv_general_dilated(
        lhs_t,
        kernel_t,
        window_strides=(1, 1),
        padding=((1, 1), (0, 0)),
        dimension_numbers=("NHWC", "HWIO", "NHWC"),
        preferred_element_type=jnp.float32,
    )
    temporal = temporal.reshape(1, frames, rows, cols, local).astype(jnp.bfloat16)
    back = lax.all_to_all(temporal, "frame", split_axis=1, concat_axis=4, tiled=True)
    per_frame = frames // frame_size
    back = back.reshape(1, per_frame, rows, cols, frame_size, rep_size, shard_width)
    back = jnp.swapaxes(back, 4, 5).reshape(1, per_frame, rows, cols, channels)
    return activations.astype(jnp.float32) + back.astype(jnp.float32) + temporal_bias


def shards(
    activations,
    spatial_weight,
    temporal_weight,
    first_gain,
    first_shift,
    spatial_bias,
    second_gain,
    second_shift,
    temporal_bias,
):
    rep_size = lax.axis_size("rep")
    frame_size = lax.axis_size("frame")
    row_size = lax.axis_size("row")
    frame_index = lax.axis_index("frame")
    row_index = lax.axis_index("row")
    channels = activations.shape[-1]
    rows = activations.shape[2]
    cols = activations.shape[3]
    width = channels // GROUPS
    shard_width = spatial_weight.shape[-1]

    spatial_shard = spatial_weight.reshape(3, 3, channels, shard_width).transpose(0, 2, 1, 3)
    spatial_w = gather_rep(spatial_shard)
    temporal_w = gather_rep(temporal_weight)
    local = rep_size * shard_width

    raw = lax.all_gather(activations, "frame", axis=1, tiled=True)
    frames = raw.shape[1]

    if row_size > 1:
        down = [(i, i + 1) for i in range(row_size - 1)]
        up = [(i + 1, i) for i in range(row_size - 1)]
        edges = jnp.concatenate(
            [
                lax.ppermute(activations[:, :, rows - 1 :], "row", down),
                lax.ppermute(activations[:, :, :1], "row", up),
            ],
            axis=2,
        )
        edges = lax.all_gather(edges, "frame", axis=1, tiled=True)
        above, below = edges[:, :, :1], edges[:, :, 1:]
    else:
        above = jnp.zeros_like(raw[:, :, :1])
        below = jnp.zeros_like(raw[:, :, :1])

    grouped = activations.astype(jnp.float32).reshape(1, -1, GROUPS, width)
    stats = jnp.concatenate(
        [jnp.sum(grouped, axis=(1, 3)), jnp.sum(grouped * grouped, axis=(1, 3))]
    )
    stats = butterfly_sum(butterfly_sum(stats, "frame"), "row")
    sums, squares = stats[:1] * 1.0, stats[1:]
    count = grouped.shape[1] * width * frame_size * row_size
    mean = sums / count
    variance = squares / count - mean * mean
    inverse = lax.rsqrt(variance + EPS)
    mean_full = jnp.repeat(mean, width, axis=1)[:, None, None, None, :]
    inverse_full = jnp.repeat(inverse, width, axis=1)[:, None, None, None, :]

    def first_norm(x):
        normed = (x.astype(jnp.float32) - mean_full) * inverse_full * first_gain + first_shift
        return silu_bf16(normed)

    first_mid = lax.optimization_barrier(first_norm(raw)[0])
    first_above = jnp.where(row_index > 0, first_norm(above), jnp.zeros((), jnp.bfloat16))[0]
    first_below = jnp.where(
        row_index < row_size - 1, first_norm(below), jnp.zeros((), jnp.bfloat16)
    )[0]

    wide = spatial_w.reshape(3, channels, 3 * local)

    def tap(field, row_tap):
        return jnp.einsum(
            "frxc,cn->frxn", field, wide[row_tap], preferred_element_type=jnp.float32
        )

    product = tap(first_mid, 1)
    product = product + jnp.pad(tap(first_mid[:, :-1], 0), ((0, 0), (1, 0), (0, 0), (0, 0)))
    product = product + jnp.pad(tap(first_mid[:, 1:], 2), ((0, 0), (0, 1), (0, 0), (0, 0)))
    product = product + jnp.pad(tap(first_above, 0), ((0, 0), (0, rows - 1), (0, 0), (0, 0)))
    product = product + jnp.pad(tap(first_below, 2), ((0, 0), (rows - 1, 0), (0, 0), (0, 0)))
    left = jnp.pad(product[:, :, :-1, :local], ((0, 0), (0, 0), (1, 0), (0, 0)))
    right = jnp.pad(product[:, :, 1:, 2 * local :], ((0, 0), (0, 0), (0, 1), (0, 0)))
    spatial = (left + product[..., local : 2 * local] + right)[None]
    spatial = spatial + local_vector(spatial_bias, frame_index, rep_size, frame_size)

    g2 = local_vector(second_gain, frame_index, rep_size, frame_size)
    s2 = local_vector(second_shift, frame_index, rep_size, frame_size)
    if shard_width % width == 0:
        grouped2 = spatial.reshape(-1, local // width, width)
        stats2 = jnp.stack(
            [jnp.sum(grouped2, axis=(0, 2)), jnp.sum(grouped2 * grouped2, axis=(0, 2))]
        )
        stats2 = pair_sum(stats2, "row")
        sums2, squares2 = stats2[0], stats2[1]
        count2 = grouped2.shape[0] * width * row_size
        mean2 = sums2 / count2
        variance2 = squares2 / count2 - mean2 * mean2
        inverse2 = lax.rsqrt(variance2 + EPS)
        mean2_full = jnp.repeat(mean2, width)
        inverse2_full = jnp.repeat(inverse2, width)
    else:
        flat = spatial.reshape(-1, local)
        csum = jnp.sum(flat, axis=0)
        csq = jnp.sum(flat * flat, axis=0)
        csum, csq = pair_sum((csum, csq), "row")
        both = lax.all_gather(jnp.stack([csum, csq]), "frame", axis=0)
        both = both.reshape(frame_size, 2, rep_size, shard_width)
        both = jnp.transpose(both, (1, 2, 0, 3)).reshape(2, GROUPS, -1)
        gsum = jnp.sum(both, axis=2)
        count2 = flat.shape[0] * row_size * width
        gmean = gsum[0] / count2
        gvar = gsum[1] / count2 - gmean * gmean
        ginv = lax.rsqrt(gvar + EPS)
        mean2_full = local_vector(jnp.repeat(gmean, width), frame_index, rep_size, frame_size)
        inverse2_full = local_vector(jnp.repeat(ginv, width), frame_index, rep_size, frame_size)
    second = silu_bf16((spatial - mean2_full) * inverse2_full * g2 + s2)

    if frame_size > 8:
        return temporal_wide(activations, second, temporal_w, temporal_bias)
    second_all = lax.all_gather(second[0], "frame", axis=0, tiled=False)
    taps = temporal_w.reshape(3, rep_size, frame_size, shard_width, local)
    total = None
    for group in range(frame_size):
        weights = taps[:, :, group].reshape(3, rep_size * shard_width, local)
        weights = weights.transpose(1, 0, 2).reshape(rep_size * shard_width, 3 * local)
        term = jnp.einsum(
            "frxc,cn->frxn", second_all[group], weights, preferred_element_type=jnp.float32
        )
        total = term if total is None else total + term
    temporal = total[..., local : 2 * local]
    if frames > 1:
        before = jnp.pad(total[:-1, ..., :local], ((1, 0), (0, 0), (0, 0), (0, 0)))
        after = jnp.pad(total[1:, ..., 2 * local :], ((0, 1), (0, 0), (0, 0), (0, 0)))
        temporal = before + temporal + after
    temporal = temporal.astype(jnp.bfloat16)

    per_frame = frames // frame_size
    pieces = []
    for shift in range(frame_size):
        target = (frame_index + shift) % frame_size
        piece = lax.dynamic_slice_in_dim(temporal, target * per_frame, per_frame, axis=0)
        if shift:
            piece = lax.ppermute(
                piece, "frame", [(k, (k + shift) % frame_size) for k in range(frame_size)]
            )
        pieces.append(piece.reshape(per_frame, rows, cols, rep_size, shard_width))
    slots = []
    for group in range(frame_size):
        wanted = (frame_index - group) % frame_size
        slot = pieces[frame_size - 1]
        for shift in range(frame_size - 2, -1, -1):
            slot = jnp.where(wanted == shift, pieces[shift], slot)
        slots.append(slot)
    result = jnp.concatenate(
        [slots[group][..., block, :] for block in range(rep_size) for group in range(frame_size)],
        axis=-1,
    )[None]
    return activations.astype(jnp.float32) + result.astype(jnp.float32) + temporal_bias


def solution(mesh):
    placed = (
        P("rep", "frame", "row", None, None),
        P(None, None, ("rep", "frame")),
        P(None, None, ("rep", "frame")),
        P(),
        P(),
        P(),
        P(),
        P(),
        P(),
    )

    return jax.shard_map(
        shards,
        mesh=mesh,
        in_specs=placed,
        out_specs=P("rep", "frame", "row", None, None),
        check_vma=False,
    )
```

```python
import numpy as np

import jax
import jax.numpy as jnp
from jax import lax
from jax.sharding import PartitionSpec as P


GROUPS = 32


EPS = 1e-05


def pair_sum(value, axis):
    if lax.axis_size(axis) == 2:
        return jax.tree.map(
            lambda v: v + lax.ppermute(v, axis, [(0, 1), (1, 0)]), value
        )
    return lax.psum(value, axis)


def butterfly_sum(value, axis):
    size = lax.axis_size(axis)
    if size & (size - 1) != 0:
        return lax.psum(value, axis)
    step = 1
    while step < size:
        pairs = [(k, k ^ step) for k in range(size)]
        value = jax.tree.map(lambda v: v + lax.ppermute(v, axis, pairs), value)
        step *= 2
    return value


def gather_rep(w):
    size = lax.axis_size("rep")
    if size != 4:
        return lax.all_gather(w, "rep", axis=w.ndim - 1, tiled=True)
    index = lax.axis_index("rep")
    across = lax.ppermute(w, "rep", [(k, k ^ 2) for k in range(size)])
    partner = lax.ppermute(w, "rep", [(k, k ^ 1) for k in range(size)])
    diagonal = lax.ppermute(across, "rep", [(k, k ^ 1) for k in range(size)])
    held = [w, partner, across, diagonal]
    blocks = []
    for position in range(size):
        offset = index ^ position
        block = held[3]
        for d in (2, 1, 0):
            block = jnp.where(offset == d, held[d], block)
        blocks.append(block)
    return jnp.concatenate(blocks, axis=-1)


def local_vector(vec, frame_index, rep_size, frame_size):
    width = vec.shape[0] // (rep_size * frame_size)
    table = vec.reshape(rep_size, frame_size, width)
    return lax.dynamic_index_in_dim(table, frame_index, axis=1, keepdims=False).reshape(-1)


def silu_bf16(normed):
    return jax.nn.silu(normed).astype(jnp.bfloat16)


def temporal_wide(activations, second, temporal_w, temporal_bias):
    rep_size = lax.axis_size("rep")
    frame_size = lax.axis_size("frame")
    channels = activations.shape[-1]
    _, frames, rows, cols, local = second.shape
    shard_width = local // rep_size
    second_all = lax.all_gather(second, "frame", axis=4, tiled=True)
    rows_order = np.arange(channels).reshape(rep_size, frame_size, shard_width)
    rows_order = rows_order.transpose(1, 0, 2).reshape(-1)
    temporal_w = temporal_w[:, rows_order, :]
    lhs_t = second_all.reshape(frames, rows * cols, channels)[None]
    kernel_t = temporal_w.reshape(3, 1, channels, local)
    temporal = lax.conv_general_dilated(
        lhs_t,
        kernel_t,
        window_strides=(1, 1),
        padding=((1, 1), (0, 0)),
        dimension_numbers=("NHWC", "HWIO", "NHWC"),
        preferred_element_type=jnp.float32,
    )
    temporal = temporal.reshape(1, frames, rows, cols, local).astype(jnp.bfloat16)
    back = lax.all_to_all(temporal, "frame", split_axis=1, concat_axis=4, tiled=True)
    per_frame = frames // frame_size
    back = back.reshape(1, per_frame, rows, cols, frame_size, rep_size, shard_width)
    back = jnp.swapaxes(back, 4, 5).reshape(1, per_frame, rows, cols, channels)
    return activations.astype(jnp.float32) + back.astype(jnp.float32) + temporal_bias


def shards(
    activations,
    spatial_weight,
    temporal_weight,
    first_gain,
    first_shift,
    spatial_bias,
    second_gain,
    second_shift,
    temporal_bias,
):
    rep_size = lax.axis_size("rep")
    frame_size = lax.axis_size("frame")
    row_size = lax.axis_size("row")
    frame_index = lax.axis_index("frame")
    row_index = lax.axis_index("row")
    channels = activations.shape[-1]
    rows = activations.shape[2]
    cols = activations.shape[3]
    width = channels // GROUPS
    shard_width = spatial_weight.shape[-1]

    spatial_shard = spatial_weight.reshape(3, 3, channels, shard_width).transpose(0, 2, 1, 3)
    spatial_w = gather_rep(spatial_shard)
    temporal_w = gather_rep(temporal_weight)
    local = rep_size * shard_width

    raw = lax.all_gather(activations, "frame", axis=1, tiled=True)
    frames = raw.shape[1]

    if row_size > 1:
        down = [(i, i + 1) for i in range(row_size - 1)]
        up = [(i + 1, i) for i in range(row_size - 1)]
        above = lax.ppermute(raw[:, :, rows - 1 :], "row", down)
        below = lax.ppermute(raw[:, :, :1], "row", up)
    else:
        above = jnp.zeros_like(raw[:, :, :1])
        below = jnp.zeros_like(raw[:, :, :1])

    grouped = activations.astype(jnp.float32).reshape(1, -1, GROUPS, width)
    stats = jnp.concatenate(
        [jnp.sum(grouped, axis=(1, 3)), jnp.sum(grouped * grouped, axis=(1, 3))]
    )
    stats = butterfly_sum(butterfly_sum(stats, "frame"), "row")
    sums, squares = stats[:1] * 1.0, stats[1:]
    count = grouped.shape[1] * width * frame_size * row_size
    mean = sums / count
    variance = squares / count - mean * mean
    inverse = lax.rsqrt(variance + EPS)
    mean_full = jnp.repeat(mean, width, axis=1)[:, None, None, None, :]
    inverse_full = jnp.repeat(inverse, width, axis=1)[:, None, None, None, :]

    def first_norm(x):
        normed = (x.astype(jnp.float32) - mean_full) * inverse_full * first_gain + first_shift
        return silu_bf16(normed)

    first_mid = lax.optimization_barrier(first_norm(raw)[0])
    first_above = jnp.where(row_index > 0, first_norm(above), jnp.zeros((), jnp.bfloat16))[0]
    first_below = jnp.where(
        row_index < row_size - 1, first_norm(below), jnp.zeros((), jnp.bfloat16)
    )[0]

    wide = spatial_w.reshape(3, channels, 3 * local)

    def tap(field, row_tap):
        return jnp.einsum(
            "frxc,cn->frxn", field, wide[row_tap], preferred_element_type=jnp.float32
        )

    product = tap(first_mid, 1)
    product = product + jnp.pad(tap(first_mid[:, :-1], 0), ((0, 0), (1, 0), (0, 0), (0, 0)))
    product = product + jnp.pad(tap(first_mid[:, 1:], 2), ((0, 0), (0, 1), (0, 0), (0, 0)))
    product = product + jnp.pad(tap(first_above, 0), ((0, 0), (0, rows - 1), (0, 0), (0, 0)))
    product = product + jnp.pad(tap(first_below, 2), ((0, 0), (rows - 1, 0), (0, 0), (0, 0)))
    left = jnp.pad(product[:, :, :-1, :local], ((0, 0), (0, 0), (1, 0), (0, 0)))
    right = jnp.pad(product[:, :, 1:, 2 * local :], ((0, 0), (0, 0), (0, 1), (0, 0)))
    spatial = (left + product[..., local : 2 * local] + right)[None]
    spatial = spatial + local_vector(spatial_bias, frame_index, rep_size, frame_size)

    g2 = local_vector(second_gain, frame_index, rep_size, frame_size)
    s2 = local_vector(second_shift, frame_index, rep_size, frame_size)
    if shard_width % width == 0:
        grouped2 = spatial.reshape(-1, local // width, width)
        stats2 = jnp.stack(
            [jnp.sum(grouped2, axis=(0, 2)), jnp.sum(grouped2 * grouped2, axis=(0, 2))]
        )
        stats2 = pair_sum(stats2, "row")
        sums2, squares2 = stats2[0], stats2[1]
        count2 = grouped2.shape[0] * width * row_size
        mean2 = sums2 / count2
        variance2 = squares2 / count2 - mean2 * mean2
        inverse2 = lax.rsqrt(variance2 + EPS)
        mean2_full = jnp.repeat(mean2, width)
        inverse2_full = jnp.repeat(inverse2, width)
    else:
        flat = spatial.reshape(-1, local)
        csum = jnp.sum(flat, axis=0)
        csq = jnp.sum(flat * flat, axis=0)
        csum, csq = pair_sum((csum, csq), "row")
        both = lax.all_gather(jnp.stack([csum, csq]), "frame", axis=0)
        both = both.reshape(frame_size, 2, rep_size, shard_width)
        both = jnp.transpose(both, (1, 2, 0, 3)).reshape(2, GROUPS, -1)
        gsum = jnp.sum(both, axis=2)
        count2 = flat.shape[0] * row_size * width
        gmean = gsum[0] / count2
        gvar = gsum[1] / count2 - gmean * gmean
        ginv = lax.rsqrt(gvar + EPS)
        mean2_full = local_vector(jnp.repeat(gmean, width), frame_index, rep_size, frame_size)
        inverse2_full = local_vector(jnp.repeat(ginv, width), frame_index, rep_size, frame_size)
    second = silu_bf16((spatial - mean2_full) * inverse2_full * g2 + s2)

    if frame_size > 8:
        return temporal_wide(activations, second, temporal_w, temporal_bias)
    second_all = lax.all_gather(second[0], "frame", axis=0, tiled=False)
    taps = temporal_w.reshape(3, rep_size, frame_size, shard_width, local)
    wide_t = taps.transpose(2, 1, 3, 0, 4).reshape(frame_size, rep_size * shard_width, 3 * local)

    def product(source, group):
        weights = lax.dynamic_index_in_dim(wide_t, group, axis=0, keepdims=False)
        return jnp.einsum("frxc,cn->frxn", source, weights, preferred_element_type=jnp.float32)

    total = product(second[0], frame_index)
    for shift in range(1, frame_size):
        group = (frame_index + shift) % frame_size
        block = lax.dynamic_index_in_dim(second_all, group, axis=0, keepdims=False)
        total = total + product(block, group)
    temporal = total[..., local : 2 * local]
    if frames > 1:
        before = jnp.pad(total[:-1, ..., :local], ((1, 0), (0, 0), (0, 0), (0, 0)))
        after = jnp.pad(total[1:, ..., 2 * local :], ((0, 1), (0, 0), (0, 0), (0, 0)))
        temporal = before + temporal + after
    temporal = temporal.astype(jnp.bfloat16)

    per_frame = frames // frame_size
    pieces = []
    for shift in range(frame_size):
        target = (frame_index + shift) % frame_size
        piece = lax.dynamic_slice_in_dim(temporal, target * per_frame, per_frame, axis=0)
        if shift:
            piece = lax.ppermute(
                piece, "frame", [(k, (k + shift) % frame_size) for k in range(frame_size)]
            )
        pieces.append(piece.reshape(per_frame, rows, cols, rep_size, shard_width))
    slots = []
    for group in range(frame_size):
        wanted = (frame_index - group) % frame_size
        slot = pieces[frame_size - 1]
        for shift in range(frame_size - 2, -1, -1):
            slot = jnp.where(wanted == shift, pieces[shift], slot)
        slots.append(slot)
    result = jnp.concatenate(
        [slots[group][..., block, :] for block in range(rep_size) for group in range(frame_size)],
        axis=-1,
    )[None]
    return activations.astype(jnp.float32) + result.astype(jnp.float32) + temporal_bias


def solution(mesh):
    placed = (
        P("rep", "frame", "row", None, None),
        P(None, None, ("rep", "frame")),
        P(None, None, ("rep", "frame")),
        P(),
        P(),
        P(),
        P(),
        P(),
        P(),
    )

    return jax.shard_map(
        shards,
        mesh=mesh,
        in_specs=placed,
        out_specs=P("rep", "frame", "row", None, None),
        check_vma=False,
    )
```

```python
import numpy as np

import jax
import jax.numpy as jnp
from jax import lax
from jax.sharding import PartitionSpec as P


GROUPS = 32


EPS = 1e-05


def pair_sum(value, axis):
    if lax.axis_size(axis) == 2:
        return jax.tree.map(
            lambda v: v + lax.ppermute(v, axis, [(0, 1), (1, 0)]), value
        )
    return lax.psum(value, axis)


def butterfly_sum(value, axis):
    size = lax.axis_size(axis)
    if size & (size - 1) != 0:
        return lax.psum(value, axis)
    step = 1
    while step < size:
        pairs = [(k, k ^ step) for k in range(size)]
        value = jax.tree.map(lambda v: v + lax.ppermute(v, axis, pairs), value)
        step *= 2
    return value


def gather_rep(w):
    size = lax.axis_size("rep")
    if size != 4:
        return lax.all_gather(w, "rep", axis=w.ndim - 1, tiled=True)
    index = lax.axis_index("rep")
    across = lax.ppermute(w, "rep", [(k, k ^ 2) for k in range(size)])
    partner = lax.ppermute(w, "rep", [(k, k ^ 1) for k in range(size)])
    diagonal = lax.ppermute(across, "rep", [(k, k ^ 1) for k in range(size)])
    held = [w, partner, across, diagonal]
    blocks = []
    for position in range(size):
        offset = index ^ position
        block = held[3]
        for d in (2, 1, 0):
            block = jnp.where(offset == d, held[d], block)
        blocks.append(block)
    return jnp.concatenate(blocks, axis=-1)


def local_vector(vec, frame_index, rep_size, frame_size):
    width = vec.shape[0] // (rep_size * frame_size)
    table = vec.reshape(rep_size, frame_size, width)
    return lax.dynamic_index_in_dim(table, frame_index, axis=1, keepdims=False).reshape(-1)


def silu_bf16(normed):
    return jax.nn.silu(normed).astype(jnp.bfloat16)


def temporal_wide(activations, second, temporal_w, temporal_bias):
    rep_size = lax.axis_size("rep")
    frame_size = lax.axis_size("frame")
    channels = activations.shape[-1]
    _, frames, rows, cols, local = second.shape
    shard_width = local // rep_size
    second_all = lax.all_gather(second, "frame", axis=4, tiled=True)
    rows_order = np.arange(channels).reshape(rep_size, frame_size, shard_width)
    rows_order = rows_order.transpose(1, 0, 2).reshape(-1)
    temporal_w = temporal_w[:, rows_order, :]
    lhs_t = second_all.reshape(frames, rows * cols, channels)[None]
    kernel_t = temporal_w.reshape(3, 1, channels, local)
    temporal = lax.conv_general_dilated(
        lhs_t,
        kernel_t,
        window_strides=(1, 1),
        padding=((1, 1), (0, 0)),
        dimension_numbers=("NHWC", "HWIO", "NHWC"),
        preferred_element_type=jnp.float32,
    )
    temporal = temporal.reshape(1, frames, rows, cols, local).astype(jnp.bfloat16)
    back = lax.all_to_all(temporal, "frame", split_axis=1, concat_axis=4, tiled=True)
    per_frame = frames // frame_size
    back = back.reshape(1, per_frame, rows, cols, frame_size, rep_size, shard_width)
    back = jnp.swapaxes(back, 4, 5).reshape(1, per_frame, rows, cols, channels)
    return activations.astype(jnp.float32) + back.astype(jnp.float32) + temporal_bias


def shards(
    activations,
    spatial_weight,
    temporal_weight,
    first_gain,
    first_shift,
    spatial_bias,
    second_gain,
    second_shift,
    temporal_bias,
):
    rep_size = lax.axis_size("rep")
    frame_size = lax.axis_size("frame")
    row_size = lax.axis_size("row")
    frame_index = lax.axis_index("frame")
    row_index = lax.axis_index("row")
    channels = activations.shape[-1]
    rows = activations.shape[2]
    cols = activations.shape[3]
    width = channels // GROUPS
    shard_width = spatial_weight.shape[-1]

    spatial_shard = spatial_weight.reshape(3, 3, channels, shard_width).transpose(0, 2, 1, 3)
    spatial_w = gather_rep(spatial_shard)
    temporal_w = gather_rep(temporal_weight)
    local = rep_size * shard_width

    raw = lax.all_gather(activations, "frame", axis=1, tiled=True)
    frames = raw.shape[1]

    edge_low, edge_high = raw[:, :, rows - 1 :], raw[:, :, :1]

    grouped = activations.astype(jnp.float32).reshape(1, -1, GROUPS, width)
    stats = jnp.concatenate(
        [jnp.sum(grouped, axis=(1, 3)), jnp.sum(grouped * grouped, axis=(1, 3))]
    )
    stats = butterfly_sum(butterfly_sum(stats, "frame"), "row")
    sums, squares = stats[:1] * 1.0, stats[1:]
    count = grouped.shape[1] * width * frame_size * row_size
    mean = sums / count
    variance = squares / count - mean * mean
    inverse = lax.rsqrt(variance + EPS)
    mean_full = jnp.repeat(mean, width, axis=1)[:, None, None, None, :]
    inverse_full = jnp.repeat(inverse, width, axis=1)[:, None, None, None, :]

    def first_norm(x):
        normed = (x.astype(jnp.float32) - mean_full) * inverse_full * first_gain + first_shift
        return silu_bf16(normed)

    first_mid = lax.optimization_barrier(first_norm(raw)[0])

    wide = spatial_w.reshape(3, channels, 3 * local)

    def tap(field, row_tap):
        return jnp.einsum(
            "frxc,cn->frxn", field, wide[row_tap], preferred_element_type=jnp.float32
        )

    product = tap(first_mid, 1)
    (edge_low, edge_high), product = lax.optimization_barrier(((edge_low, edge_high), product))
    if row_size > 1:
        down = [(i, i + 1) for i in range(row_size - 1)]
        up = [(i + 1, i) for i in range(row_size - 1)]
        above = lax.ppermute(edge_low, "row", down)
        below = lax.ppermute(edge_high, "row", up)
    else:
        above = jnp.zeros_like(edge_low)
        below = jnp.zeros_like(edge_high)
    first_above = jnp.where(row_index > 0, first_norm(above), jnp.zeros((), jnp.bfloat16))[0]
    first_below = jnp.where(
        row_index < row_size - 1, first_norm(below), jnp.zeros((), jnp.bfloat16)
    )[0]
    product = product + jnp.pad(tap(first_mid[:, :-1], 0), ((0, 0), (1, 0), (0, 0), (0, 0)))
    product = product + jnp.pad(tap(first_mid[:, 1:], 2), ((0, 0), (0, 1), (0, 0), (0, 0)))
    product = product + jnp.pad(tap(first_above, 0), ((0, 0), (0, rows - 1), (0, 0), (0, 0)))
    product = product + jnp.pad(tap(first_below, 2), ((0, 0), (rows - 1, 0), (0, 0), (0, 0)))
    left = jnp.pad(product[:, :, :-1, :local], ((0, 0), (0, 0), (1, 0), (0, 0)))
    right = jnp.pad(product[:, :, 1:, 2 * local :], ((0, 0), (0, 0), (0, 1), (0, 0)))
    spatial = (left + product[..., local : 2 * local] + right)[None]
    spatial = spatial + local_vector(spatial_bias, frame_index, rep_size, frame_size)

    g2 = local_vector(second_gain, frame_index, rep_size, frame_size)
    s2 = local_vector(second_shift, frame_index, rep_size, frame_size)
    if shard_width % width == 0:
        grouped2 = spatial.reshape(-1, local // width, width)
        stats2 = jnp.stack(
            [jnp.sum(grouped2, axis=(0, 2)), jnp.sum(grouped2 * grouped2, axis=(0, 2))]
        )
        stats2 = pair_sum(stats2, "row")
        sums2, squares2 = stats2[0], stats2[1]
        count2 = grouped2.shape[0] * width * row_size
        mean2 = sums2 / count2
        variance2 = squares2 / count2 - mean2 * mean2
        inverse2 = lax.rsqrt(variance2 + EPS)
        mean2_full = jnp.repeat(mean2, width)
        inverse2_full = jnp.repeat(inverse2, width)
    else:
        flat = spatial.reshape(-1, local)
        csum = jnp.sum(flat, axis=0)
        csq = jnp.sum(flat * flat, axis=0)
        csum, csq = pair_sum((csum, csq), "row")
        both = lax.all_gather(jnp.stack([csum, csq]), "frame", axis=0)
        both = both.reshape(frame_size, 2, rep_size, shard_width)
        both = jnp.transpose(both, (1, 2, 0, 3)).reshape(2, GROUPS, -1)
        gsum = jnp.sum(both, axis=2)
        count2 = flat.shape[0] * row_size * width
        gmean = gsum[0] / count2
        gvar = gsum[1] / count2 - gmean * gmean
        ginv = lax.rsqrt(gvar + EPS)
        mean2_full = local_vector(jnp.repeat(gmean, width), frame_index, rep_size, frame_size)
        inverse2_full = local_vector(jnp.repeat(ginv, width), frame_index, rep_size, frame_size)
    second = silu_bf16((spatial - mean2_full) * inverse2_full * g2 + s2)

    if frame_size > 8:
        return temporal_wide(activations, second, temporal_w, temporal_bias)
    second_all = lax.all_gather(second[0], "frame", axis=0, tiled=False)
    taps = temporal_w.reshape(3, rep_size, frame_size, shard_width, local)
    wide_t = taps.transpose(2, 1, 3, 0, 4).reshape(frame_size, rep_size * shard_width, 3 * local)

    def product(source, group):
        weights = lax.dynamic_index_in_dim(wide_t, group, axis=0, keepdims=False)
        return jnp.einsum("frxc,cn->frxn", source, weights, preferred_element_type=jnp.float32)

    total = product(second[0], frame_index)
    for shift in range(1, frame_size):
        group = (frame_index + shift) % frame_size
        block = lax.dynamic_index_in_dim(second_all, group, axis=0, keepdims=False)
        total = total + product(block, group)
    temporal = total[..., local : 2 * local]
    if frames > 1:
        before = jnp.pad(total[:-1, ..., :local], ((1, 0), (0, 0), (0, 0), (0, 0)))
        after = jnp.pad(total[1:, ..., 2 * local :], ((0, 1), (0, 0), (0, 0), (0, 0)))
        temporal = before + temporal + after
    temporal = temporal.astype(jnp.bfloat16)

    per_frame = frames // frame_size
    pieces = []
    for shift in range(frame_size):
        target = (frame_index + shift) % frame_size
        piece = lax.dynamic_slice_in_dim(temporal, target * per_frame, per_frame, axis=0)
        if shift:
            piece = lax.ppermute(
                piece, "frame", [(k, (k + shift) % frame_size) for k in range(frame_size)]
            )
        pieces.append(piece.reshape(per_frame, rows, cols, rep_size, shard_width))
    slots = []
    for group in range(frame_size):
        wanted = (frame_index - group) % frame_size
        slot = pieces[frame_size - 1]
        for shift in range(frame_size - 2, -1, -1):
            slot = jnp.where(wanted == shift, pieces[shift], slot)
        slots.append(slot)
    result = jnp.concatenate(
        [slots[group][..., block, :] for block in range(rep_size) for group in range(frame_size)],
        axis=-1,
    )[None]
    return activations.astype(jnp.float32) + result.astype(jnp.float32) + temporal_bias


def solution(mesh):
    placed = (
        P("rep", "frame", "row", None, None),
        P(None, None, ("rep", "frame")),
        P(None, None, ("rep", "frame")),
        P(),
        P(),
        P(),
        P(),
        P(),
        P(),
    )

    return jax.shard_map(
        shards,
        mesh=mesh,
        in_specs=placed,
        out_specs=P("rep", "frame", "row", None, None),
        check_vma=False,
    )
```

```python
import numpy as np

import jax
import jax.numpy as jnp
from jax import lax
from jax.sharding import PartitionSpec as P


GROUPS = 32


EPS = 1e-05


def pair_sum(value, axis):
    if lax.axis_size(axis) == 2:
        return jax.tree.map(
            lambda v: v + lax.ppermute(v, axis, [(0, 1), (1, 0)]), value
        )
    return lax.psum(value, axis)


def butterfly_sum(value, axis):
    size = lax.axis_size(axis)
    if size & (size - 1) != 0:
        return lax.psum(value, axis)
    step = 1
    while step < size:
        pairs = [(k, k ^ step) for k in range(size)]
        value = jax.tree.map(lambda v: v + lax.ppermute(v, axis, pairs), value)
        step *= 2
    return value


def gather_rep(w):
    size = lax.axis_size("rep")
    if size != 4:
        return lax.all_gather(w, "rep", axis=w.ndim - 1, tiled=True)
    index = lax.axis_index("rep")
    across = lax.ppermute(w, "rep", [(k, k ^ 2) for k in range(size)])
    partner = lax.ppermute(w, "rep", [(k, k ^ 1) for k in range(size)])
    diagonal = lax.ppermute(across, "rep", [(k, k ^ 1) for k in range(size)])
    held = [w, partner, across, diagonal]
    blocks = []
    for position in range(size):
        offset = index ^ position
        block = held[3]
        for d in (2, 1, 0):
            block = jnp.where(offset == d, held[d], block)
        blocks.append(block)
    return jnp.concatenate(blocks, axis=-1)


def local_vector(vec, frame_index, rep_size, frame_size):
    width = vec.shape[0] // (rep_size * frame_size)
    table = vec.reshape(rep_size, frame_size, width)
    return lax.dynamic_index_in_dim(table, frame_index, axis=1, keepdims=False).reshape(-1)


def silu_bf16(normed):
    return jax.nn.silu(normed).astype(jnp.bfloat16)


def temporal_wide(activations, second, temporal_w, temporal_bias):
    rep_size = lax.axis_size("rep")
    frame_size = lax.axis_size("frame")
    channels = activations.shape[-1]
    _, frames, rows, cols, local = second.shape
    shard_width = local // rep_size
    second_all = lax.all_gather(second, "frame", axis=4, tiled=True)
    rows_order = np.arange(channels).reshape(rep_size, frame_size, shard_width)
    rows_order = rows_order.transpose(1, 0, 2).reshape(-1)
    temporal_w = temporal_w[:, rows_order, :]
    lhs_t = second_all.reshape(frames, rows * cols, channels)[None]
    kernel_t = temporal_w.reshape(3, 1, channels, local)
    temporal = lax.conv_general_dilated(
        lhs_t,
        kernel_t,
        window_strides=(1, 1),
        padding=((1, 1), (0, 0)),
        dimension_numbers=("NHWC", "HWIO", "NHWC"),
        preferred_element_type=jnp.float32,
    )
    temporal = temporal.reshape(1, frames, rows, cols, local).astype(jnp.bfloat16)
    back = lax.all_to_all(temporal, "frame", split_axis=1, concat_axis=4, tiled=True)
    per_frame = frames // frame_size
    back = back.reshape(1, per_frame, rows, cols, frame_size, rep_size, shard_width)
    back = jnp.swapaxes(back, 4, 5).reshape(1, per_frame, rows, cols, channels)
    return activations.astype(jnp.float32) + back.astype(jnp.float32) + temporal_bias


def shards(
    activations,
    spatial_weight,
    temporal_weight,
    first_gain,
    first_shift,
    spatial_bias,
    second_gain,
    second_shift,
    temporal_bias,
):
    rep_size = lax.axis_size("rep")
    frame_size = lax.axis_size("frame")
    row_size = lax.axis_size("row")
    frame_index = lax.axis_index("frame")
    row_index = lax.axis_index("row")
    channels = activations.shape[-1]
    rows = activations.shape[2]
    cols = activations.shape[3]
    width = channels // GROUPS
    shard_width = spatial_weight.shape[-1]

    spatial_shard = spatial_weight.reshape(3, 3, channels, shard_width).transpose(0, 2, 1, 3)
    spatial_w = gather_rep(spatial_shard)
    temporal_w = gather_rep(temporal_weight)
    local = rep_size * shard_width

    raw = lax.all_gather(activations, "frame", axis=1, tiled=True)
    frames = raw.shape[1]

    if row_size > 1:
        down = [(i, i + 1) for i in range(row_size - 1)]
        up = [(i + 1, i) for i in range(row_size - 1)]
        above = lax.ppermute(raw[:, :, rows - 1 :], "row", down)
        below = lax.ppermute(raw[:, :, :1], "row", up)
    else:
        above = jnp.zeros_like(raw[:, :, :1])
        below = jnp.zeros_like(raw[:, :, :1])

    grouped = activations.astype(jnp.float32).reshape(1, -1, GROUPS, width)
    stats = jnp.concatenate(
        [jnp.sum(grouped, axis=(1, 3)), jnp.sum(grouped * grouped, axis=(1, 3))]
    )
    stats = butterfly_sum(butterfly_sum(stats, "frame"), "row")
    sums, squares = stats[:1] * 1.0, stats[1:]
    count = grouped.shape[1] * width * frame_size * row_size
    mean = sums / count
    variance = squares / count - mean * mean
    inverse = lax.rsqrt(variance + EPS)
    mean_full = jnp.repeat(mean, width, axis=1)[:, None, None, None, :]
    inverse_full = jnp.repeat(inverse, width, axis=1)[:, None, None, None, :]

    def first_norm(x):
        normed = (x.astype(jnp.float32) - mean_full) * inverse_full * first_gain + first_shift
        return silu_bf16(normed)

    first_mid = lax.optimization_barrier(first_norm(raw)[0])
    first_above = jnp.where(row_index > 0, first_norm(above), jnp.zeros((), jnp.bfloat16))[0]
    first_below = jnp.where(
        row_index < row_size - 1, first_norm(below), jnp.zeros((), jnp.bfloat16)
    )[0]

    wide = spatial_w.reshape(3, channels, 3 * local)

    def tap(field, row_tap):
        return jnp.einsum(
            "frxc,cn->frxn", field, wide[row_tap], preferred_element_type=jnp.float32
        )

    product = tap(first_mid, 1)
    product = product + tap(jnp.concatenate([first_above, first_mid[:, :-1]], axis=1), 0)
    product = product + tap(jnp.concatenate([first_mid[:, 1:], first_below], axis=1), 2)
    left = jnp.pad(product[:, :, :-1, :local], ((0, 0), (0, 0), (1, 0), (0, 0)))
    right = jnp.pad(product[:, :, 1:, 2 * local :], ((0, 0), (0, 0), (0, 1), (0, 0)))
    spatial = (left + product[..., local : 2 * local] + right)[None]
    spatial = spatial + local_vector(spatial_bias, frame_index, rep_size, frame_size)

    g2 = local_vector(second_gain, frame_index, rep_size, frame_size)
    s2 = local_vector(second_shift, frame_index, rep_size, frame_size)
    if shard_width % width == 0:
        grouped2 = spatial.reshape(-1, local // width, width)
        stats2 = jnp.stack(
            [jnp.sum(grouped2, axis=(0, 2)), jnp.sum(grouped2 * grouped2, axis=(0, 2))]
        )
        stats2 = pair_sum(stats2, "row")
        sums2, squares2 = stats2[0], stats2[1]
        count2 = grouped2.shape[0] * width * row_size
        mean2 = sums2 / count2
        variance2 = squares2 / count2 - mean2 * mean2
        inverse2 = lax.rsqrt(variance2 + EPS)
        mean2_full = jnp.repeat(mean2, width)
        inverse2_full = jnp.repeat(inverse2, width)
    else:
        flat = spatial.reshape(-1, local)
        csum = jnp.sum(flat, axis=0)
        csq = jnp.sum(flat * flat, axis=0)
        csum, csq = pair_sum((csum, csq), "row")
        both = lax.all_gather(jnp.stack([csum, csq]), "frame", axis=0)
        both = both.reshape(frame_size, 2, rep_size, shard_width)
        both = jnp.transpose(both, (1, 2, 0, 3)).reshape(2, GROUPS, -1)
        gsum = jnp.sum(both, axis=2)
        count2 = flat.shape[0] * row_size * width
        gmean = gsum[0] / count2
        gvar = gsum[1] / count2 - gmean * gmean
        ginv = lax.rsqrt(gvar + EPS)
        mean2_full = local_vector(jnp.repeat(gmean, width), frame_index, rep_size, frame_size)
        inverse2_full = local_vector(jnp.repeat(ginv, width), frame_index, rep_size, frame_size)
    second = silu_bf16((spatial - mean2_full) * inverse2_full * g2 + s2)

    if frame_size > 8:
        return temporal_wide(activations, second, temporal_w, temporal_bias)
    second_all = lax.all_gather(second[0], "frame", axis=0, tiled=False)
    taps = temporal_w.reshape(3, rep_size, frame_size, shard_width, local)
    wide_t = taps.transpose(2, 1, 3, 0, 4).reshape(frame_size, rep_size * shard_width, 3 * local)

    def product(source, group):
        weights = lax.dynamic_index_in_dim(wide_t, group, axis=0, keepdims=False)
        return jnp.einsum("frxc,cn->frxn", source, weights, preferred_element_type=jnp.float32)

    total = product(second[0], frame_index)
    for shift in range(1, frame_size):
        group = (frame_index + shift) % frame_size
        block = lax.dynamic_index_in_dim(second_all, group, axis=0, keepdims=False)
        total = total + product(block, group)
    temporal = total[..., local : 2 * local]
    if frames > 1:
        before = jnp.pad(total[:-1, ..., :local], ((1, 0), (0, 0), (0, 0), (0, 0)))
        after = jnp.pad(total[1:, ..., 2 * local :], ((0, 1), (0, 0), (0, 0), (0, 0)))
        temporal = before + temporal + after
    temporal = temporal.astype(jnp.bfloat16)

    per_frame = frames // frame_size
    pieces = []
    for shift in range(frame_size):
        target = (frame_index + shift) % frame_size
        piece = lax.dynamic_slice_in_dim(temporal, target * per_frame, per_frame, axis=0)
        if shift:
            piece = lax.ppermute(
                piece, "frame", [(k, (k + shift) % frame_size) for k in range(frame_size)]
            )
        pieces.append(piece.reshape(per_frame, rows, cols, rep_size, shard_width))
    slots = []
    for group in range(frame_size):
        wanted = (frame_index - group) % frame_size
        slot = pieces[frame_size - 1]
        for shift in range(frame_size - 2, -1, -1):
            slot = jnp.where(wanted == shift, pieces[shift], slot)
        slots.append(slot)
    result = jnp.concatenate(
        [slots[group][..., block, :] for block in range(rep_size) for group in range(frame_size)],
        axis=-1,
    )[None]
    return activations.astype(jnp.float32) + result.astype(jnp.float32) + temporal_bias


def solution(mesh):
    placed = (
        P("rep", "frame", "row", None, None),
        P(None, None, ("rep", "frame")),
        P(None, None, ("rep", "frame")),
        P(),
        P(),
        P(),
        P(),
        P(),
        P(),
    )

    return jax.shard_map(
        shards,
        mesh=mesh,
        in_specs=placed,
        out_specs=P("rep", "frame", "row", None, None),
        check_vma=False,
    )
```

```python
import numpy as np

import jax
import jax.numpy as jnp
from jax import lax
from jax.sharding import PartitionSpec as P


GROUPS = 32


EPS = 1e-05


def pair_sum(value, axis):
    if lax.axis_size(axis) == 2:
        return jax.tree.map(
            lambda v: v + lax.ppermute(v, axis, [(0, 1), (1, 0)]), value
        )
    return lax.psum(value, axis)


def butterfly_sum(value, axis):
    size = lax.axis_size(axis)
    if size & (size - 1) != 0:
        return lax.psum(value, axis)
    step = 1
    while step < size:
        pairs = [(k, k ^ step) for k in range(size)]
        value = jax.tree.map(lambda v: v + lax.ppermute(v, axis, pairs), value)
        step *= 2
    return value


def gather_rep(w):
    size = lax.axis_size("rep")
    if size != 4:
        return lax.all_gather(w, "rep", axis=w.ndim - 1, tiled=True)
    index = lax.axis_index("rep")
    across = lax.ppermute(w, "rep", [(k, k ^ 2) for k in range(size)])
    partner = lax.ppermute(w, "rep", [(k, k ^ 1) for k in range(size)])
    diagonal = lax.ppermute(across, "rep", [(k, k ^ 1) for k in range(size)])
    held = [w, partner, across, diagonal]
    blocks = []
    for position in range(size):
        offset = index ^ position
        block = held[3]
        for d in (2, 1, 0):
            block = jnp.where(offset == d, held[d], block)
        blocks.append(block)
    return jnp.concatenate(blocks, axis=-1)


def local_vector(vec, frame_index, rep_size, frame_size):
    width = vec.shape[0] // (rep_size * frame_size)
    table = vec.reshape(rep_size, frame_size, width)
    return lax.dynamic_index_in_dim(table, frame_index, axis=1, keepdims=False).reshape(-1)


def silu_bf16(normed):
    return jax.nn.silu(normed).astype(jnp.bfloat16)


def temporal_wide(activations, second, temporal_w, temporal_bias):
    rep_size = lax.axis_size("rep")
    frame_size = lax.axis_size("frame")
    channels = activations.shape[-1]
    _, frames, rows, cols, local = second.shape
    shard_width = local // rep_size
    second_all = lax.all_gather(second, "frame", axis=4, tiled=True)
    rows_order = np.arange(channels).reshape(rep_size, frame_size, shard_width)
    rows_order = rows_order.transpose(1, 0, 2).reshape(-1)
    temporal_w = temporal_w[:, rows_order, :]
    lhs_t = second_all.reshape(frames, rows * cols, channels)[None]
    kernel_t = temporal_w.reshape(3, 1, channels, local)
    temporal = lax.conv_general_dilated(
        lhs_t,
        kernel_t,
        window_strides=(1, 1),
        padding=((1, 1), (0, 0)),
        dimension_numbers=("NHWC", "HWIO", "NHWC"),
        preferred_element_type=jnp.float32,
    )
    temporal = temporal.reshape(1, frames, rows, cols, local).astype(jnp.bfloat16)
    back = lax.all_to_all(temporal, "frame", split_axis=1, concat_axis=4, tiled=True)
    per_frame = frames // frame_size
    back = back.reshape(1, per_frame, rows, cols, frame_size, rep_size, shard_width)
    back = jnp.swapaxes(back, 4, 5).reshape(1, per_frame, rows, cols, channels)
    return activations.astype(jnp.float32) + back.astype(jnp.float32) + temporal_bias


def shards(
    activations,
    spatial_weight,
    temporal_weight,
    first_gain,
    first_shift,
    spatial_bias,
    second_gain,
    second_shift,
    temporal_bias,
):
    rep_size = lax.axis_size("rep")
    frame_size = lax.axis_size("frame")
    row_size = lax.axis_size("row")
    frame_index = lax.axis_index("frame")
    channels = activations.shape[-1]
    rows = activations.shape[2]
    cols = activations.shape[3]
    width = channels // GROUPS
    shard_width = spatial_weight.shape[-1]

    spatial_shard = spatial_weight.reshape(3, 3, channels, shard_width).transpose(0, 2, 1, 3)
    spatial_w = gather_rep(spatial_shard)
    temporal_w = gather_rep(temporal_weight)
    local = rep_size * shard_width

    raw = lax.all_gather(activations, "frame", axis=1, tiled=True)
    frames = raw.shape[1]


    grouped = activations.astype(jnp.float32).reshape(1, -1, GROUPS, width)
    stats = jnp.concatenate(
        [jnp.sum(grouped, axis=(1, 3)), jnp.sum(grouped * grouped, axis=(1, 3))]
    )
    stats = butterfly_sum(butterfly_sum(stats, "frame"), "row")
    sums, squares = stats[:1] * 1.0, stats[1:]
    count = grouped.shape[1] * width * frame_size * row_size
    mean = sums / count
    variance = squares / count - mean * mean
    inverse = lax.rsqrt(variance + EPS)
    mean_full = jnp.repeat(mean, width, axis=1)[:, None, None, None, :]
    inverse_full = jnp.repeat(inverse, width, axis=1)[:, None, None, None, :]

    def first_norm(x):
        normed = (x.astype(jnp.float32) - mean_full) * inverse_full * first_gain + first_shift
        return silu_bf16(normed)

    first_mid = lax.optimization_barrier(first_norm(raw)[0])
    if row_size > 1:
        down = [(i, i + 1) for i in range(row_size - 1)]
        up = [(i + 1, i) for i in range(row_size - 1)]
        first_above = lax.ppermute(first_mid[:, rows - 1 :], "row", down)
        first_below = lax.ppermute(first_mid[:, :1], "row", up)
    else:
        first_above = jnp.zeros_like(first_mid[:, :1])
        first_below = jnp.zeros_like(first_mid[:, :1])

    wide = spatial_w.reshape(3, channels, 3 * local)

    def tap(field, row_tap):
        return jnp.einsum(
            "frxc,cn->frxn", field, wide[row_tap], preferred_element_type=jnp.float32
        )

    product = tap(first_mid, 1)
    product = product + jnp.pad(tap(first_mid[:, :-1], 0), ((0, 0), (1, 0), (0, 0), (0, 0)))
    product = product + jnp.pad(tap(first_mid[:, 1:], 2), ((0, 0), (0, 1), (0, 0), (0, 0)))
    product = product + jnp.pad(tap(first_above, 0), ((0, 0), (0, rows - 1), (0, 0), (0, 0)))
    product = product + jnp.pad(tap(first_below, 2), ((0, 0), (rows - 1, 0), (0, 0), (0, 0)))
    left = jnp.pad(product[:, :, :-1, :local], ((0, 0), (0, 0), (1, 0), (0, 0)))
    right = jnp.pad(product[:, :, 1:, 2 * local :], ((0, 0), (0, 0), (0, 1), (0, 0)))
    spatial = (left + product[..., local : 2 * local] + right)[None]
    spatial = spatial + local_vector(spatial_bias, frame_index, rep_size, frame_size)

    g2 = local_vector(second_gain, frame_index, rep_size, frame_size)
    s2 = local_vector(second_shift, frame_index, rep_size, frame_size)
    if shard_width % width == 0:
        grouped2 = spatial.reshape(-1, local // width, width)
        stats2 = jnp.stack(
            [jnp.sum(grouped2, axis=(0, 2)), jnp.sum(grouped2 * grouped2, axis=(0, 2))]
        )
        stats2 = pair_sum(stats2, "row")
        sums2, squares2 = stats2[0], stats2[1]
        count2 = grouped2.shape[0] * width * row_size
        mean2 = sums2 / count2
        variance2 = squares2 / count2 - mean2 * mean2
        inverse2 = lax.rsqrt(variance2 + EPS)
        mean2_full = jnp.repeat(mean2, width)
        inverse2_full = jnp.repeat(inverse2, width)
    else:
        flat = spatial.reshape(-1, local)
        csum = jnp.sum(flat, axis=0)
        csq = jnp.sum(flat * flat, axis=0)
        csum, csq = pair_sum((csum, csq), "row")
        both = lax.all_gather(jnp.stack([csum, csq]), "frame", axis=0)
        both = both.reshape(frame_size, 2, rep_size, shard_width)
        both = jnp.transpose(both, (1, 2, 0, 3)).reshape(2, GROUPS, -1)
        gsum = jnp.sum(both, axis=2)
        count2 = flat.shape[0] * row_size * width
        gmean = gsum[0] / count2
        gvar = gsum[1] / count2 - gmean * gmean
        ginv = lax.rsqrt(gvar + EPS)
        mean2_full = local_vector(jnp.repeat(gmean, width), frame_index, rep_size, frame_size)
        inverse2_full = local_vector(jnp.repeat(ginv, width), frame_index, rep_size, frame_size)
    second = silu_bf16((spatial - mean2_full) * inverse2_full * g2 + s2)

    if frame_size > 8:
        return temporal_wide(activations, second, temporal_w, temporal_bias)
    second_all = lax.all_gather(second[0], "frame", axis=0, tiled=False)
    taps = temporal_w.reshape(3, rep_size, frame_size, shard_width, local)
    wide_t = taps.transpose(2, 1, 3, 0, 4).reshape(frame_size, rep_size * shard_width, 3 * local)

    def product(source, group):
        weights = lax.dynamic_index_in_dim(wide_t, group, axis=0, keepdims=False)
        return jnp.einsum("frxc,cn->frxn", source, weights, preferred_element_type=jnp.float32)

    total = product(second[0], frame_index)
    for shift in range(1, frame_size):
        group = (frame_index + shift) % frame_size
        block = lax.dynamic_index_in_dim(second_all, group, axis=0, keepdims=False)
        total = total + product(block, group)
    temporal = total[..., local : 2 * local]
    if frames > 1:
        before = jnp.pad(total[:-1, ..., :local], ((1, 0), (0, 0), (0, 0), (0, 0)))
        after = jnp.pad(total[1:, ..., 2 * local :], ((0, 1), (0, 0), (0, 0), (0, 0)))
        temporal = before + temporal + after
    temporal = temporal.astype(jnp.bfloat16)

    per_frame = frames // frame_size
    pieces = []
    for shift in range(frame_size):
        target = (frame_index + shift) % frame_size
        piece = lax.dynamic_slice_in_dim(temporal, target * per_frame, per_frame, axis=0)
        if shift:
            piece = lax.ppermute(
                piece, "frame", [(k, (k + shift) % frame_size) for k in range(frame_size)]
            )
        pieces.append(piece.reshape(per_frame, rows, cols, rep_size, shard_width))
    slots = []
    for group in range(frame_size):
        wanted = (frame_index - group) % frame_size
        slot = pieces[frame_size - 1]
        for shift in range(frame_size - 2, -1, -1):
            slot = jnp.where(wanted == shift, pieces[shift], slot)
        slots.append(slot)
    result = jnp.concatenate(
        [slots[group][..., block, :] for block in range(rep_size) for group in range(frame_size)],
        axis=-1,
    )[None]
    return activations.astype(jnp.float32) + result.astype(jnp.float32) + temporal_bias


def solution(mesh):
    placed = (
        P("rep", "frame", "row", None, None),
        P(None, None, ("rep", "frame")),
        P(None, None, ("rep", "frame")),
        P(),
        P(),
        P(),
        P(),
        P(),
        P(),
    )

    return jax.shard_map(
        shards,
        mesh=mesh,
        in_specs=placed,
        out_specs=P("rep", "frame", "row", None, None),
        check_vma=False,
    )
```
